256 devices in a mesh: kv: 4 (over y), ctx: 64 (over x, z, core).
Axes of the slice: x: 4, y: 4, z: 8, core: 2. Of those that a mesh axis runs over, the one named last changes fastest.
Arguments:
- queries: bfloat16 [1024, 8192], P('ctx', 'kv'), may hold values from -8 to 8
- key_cache: bfloat16 [262144, 1024], P('ctx', 'kv'), may hold values from -8 to 8
- value_cache: bfloat16 [262144, 1024], P('ctx', 'kv'), may hold values from -6 to 6
- blocks: int32 [8, 8, 256], replicated, may hold values from 0 to 2047, as said below
- out_weight: bfloat16 [8192, 8192], P('kv', 'ctx'), may hold values from -0.0625 to 0.0625
Outputs:
- attended: bfloat16 [1024, 8192], P('kv', 'ctx')
The draws below stay inside these ranges and needn't reach their ends.
Inputs may be any that keep to these rules, and one draw needn't show every extreme that they name: blocks[b, h, :] lists 256 distinct key blocks in ascending order, none after block 2040 + b and always that block itself; each list names at most 7 of one cache device's 32 blocks, and a quarter of the 64 cache devices get 1, 3, 5 and 7 of its blocks each.
All inputs are finite; a program needn't handle non-finite values.
Results may differ from the reference program's by a relative error of at most 0.012.
Values may be sent and summed in bfloat16 or wider, within the bound.
No kernel may reach another device: no remote copies, remote signals or barrier semaphores. Data moves between devices by JAX's collectives and lax.ppermute only.
A program may use at most 64 MiB of HBM per device.

```python
import math
import jax
import jax.numpy as jnp
from jax import lax

D = 8192
HQ = 64
KVH = 8
HD = 128
BLK = 128
QBLK = 8
MOST = 7
BPS = 32
CTX_DEV = 4096
CTX = 262144
NKB = 2048
SEL = 256
QTOK = 1024
N_CTX = 64


def draw_queries(key, part):
    shape = (QTOK, HQ * HD)
    values = jax.random.truncated_normal(jax.random.fold_in(key, 1), -6.0, 6.0, shape, jnp.float32)
    return values.astype(jnp.bfloat16)


def draw_key_cache(key, part):
    shape = (CTX, KVH * HD)
    values = jax.random.truncated_normal(jax.random.fold_in(key, 2), -6.0, 6.0, shape, jnp.float32)
    return values.astype(jnp.bfloat16)


def draw_blocks(key, part):
    shards = N_CTX
    base = jax.random.fold_in(key, 21)
    jitter = jax.random.randint(jax.random.fold_in(base, 1), (QBLK, KVH, shards), 0, shards // 2 + 1)
    order = jnp.arange(shards, dtype=jnp.int32)
    ranking = (order + jitter) * shards + order
    rank = jnp.argsort(jnp.argsort(ranking, axis=-1), axis=-1)
    counts = 1 + 2 * (4 * rank // shards)
    local = jnp.arange(BPS, dtype=jnp.int32)
    globals_here = order[:, None] * BPS + local[None, :]
    limit = NKB - QBLK + jnp.arange(QBLK, dtype=jnp.int32)[:, None, None, None]
    candidate = jax.random.randint(jax.random.fold_in(base, 2), (QBLK, KVH, shards, BPS), 0, 1 << 20) * BPS + local
    candidate = jnp.where(globals_here[None, None] == limit, 1 << 30, candidate)
    candidate = jnp.where(globals_here[None, None] > limit, -1, candidate)
    unused, top_index = lax.top_k(candidate, MOST)
    picked = order[:, None] * BPS + top_index
    keep = jnp.arange(MOST, dtype=jnp.int32) < counts[..., None]
    picked = jnp.where(keep, picked, NKB)
    flat = jnp.sort(picked.reshape(QBLK, KVH, shards * MOST), axis=-1)
    return flat[..., :SEL].astype(jnp.int32)


def steps_of(key, shape, cuts, smallest, high):
    level, own = 1.0, jax.random.fold_in(key, 6)
    for axis_at, shards_of in cuts:
        heights = jnp.exp(jax.random.uniform(jax.random.fold_in(own, axis_at), (shards_of,), jnp.float32, smallest / len(cuts), high / len(cuts)))
        level = level * jnp.repeat(heights, shape[axis_at] // shards_of).reshape([-1 if axis == axis_at else 1 for axis in range(len(shape))])
    return level


def normal_values(own_key, dims, deviation, reach, cuts=(), kind=jnp.bfloat16):
    factor_of = steps_of(own_key, dims, cuts, -0.22, 0.18) if cuts else 1.0
    array = jax.random.normal(own_key, dims, jnp.float32) * deviation * factor_of
    return jnp.minimum(jnp.maximum(array, -reach), reach).astype(kind)


def setup_inputs(seed: int = 0) -> dict:
    keys = jax.random.split(jax.random.key(seed), 6)
    queries = draw_queries(jax.random.fold_in(keys[5], 71), 0)
    key_cache = draw_key_cache(jax.random.fold_in(keys[5], 71), 0)
    value_cache = normal_values(keys[2], (CTX, KVH * HD), 1.0, 6.0, ((0, 64), (1, 4)))
    blocks = draw_blocks(jax.random.fold_in(keys[5], 71), 0)
    out_weight = normal_values(keys[4], (HQ * HD, D), (HQ * HD) ** -0.5, 0.0625, ((0, 4), (1, 64)))
    return dict(queries=queries, key_cache=key_cache, value_cache=value_cache, blocks=blocks, out_weight=out_weight)


def shard_partials(queries_all, key_shard, value_shard, block_lists, shard_first, total_keys, head_count):
    query_tokens = queries_all.shape[0]
    blocks_here = key_shard.shape[0] // BLK
    group_size = queries_all.shape[1] // (head_count * HD)
    score_scale = 1.0 / math.sqrt(HD)
    below = lax.optimization_barrier(jnp.sum((block_lists < shard_first).astype(jnp.int32), axis=-1))
    inside = lax.optimization_barrier(jnp.sum(((block_lists >= shard_first) & (block_lists < shard_first + blocks_here)).astype(jnp.int32), axis=-1))
    slot_ids = jnp.arange(MOST, dtype=jnp.int32)
    places = jnp.clip(below[..., None] + slot_ids, 0, block_lists.shape[-1] - 1).astype(jnp.int32)
    picked = jnp.take_along_axis(block_lists, places, axis=-1) - shard_first
    usable = slot_ids < inside[..., None]
    picked = jnp.where(usable, picked, 0).astype(jnp.int32)
    key_blocks = key_shard.reshape(blocks_here, BLK, head_count, HD)
    value_blocks = value_shard.reshape(blocks_here, BLK, head_count, HD)
    offsets = jnp.arange(BLK, dtype=jnp.int32)

    def one_block(inputs):
        block_index, picked_now, usable_now = inputs
        rows_here = lax.dynamic_slice_in_dim(queries_all, block_index * BLK, BLK, 0)
        rows_here = rows_here.reshape(BLK, head_count, group_size, HD).astype(jnp.float32)
        query_pos = total_keys - query_tokens + block_index * BLK + offsets
        head_outputs, head_peaks, head_totals = ([], [], [])
        for head_index in range(head_count):
            chosen = picked_now[head_index]
            keys_taken = key_blocks[chosen, :, head_index, :].reshape(MOST * BLK, HD).astype(jnp.float32)
            values_taken = value_blocks[chosen, :, head_index, :].reshape(MOST * BLK, HD).astype(jnp.float32)
            key_pos = ((shard_first + chosen)[:, None] * BLK + offsets[None, :]).reshape(MOST * BLK)
            live_keys = jnp.repeat(usable_now[head_index], BLK)
            allowed = live_keys[None, :] & (key_pos[None, :] <= query_pos[:, None])
            scores = jnp.einsum('rgd,kd->rgk', rows_here[:, head_index], keys_taken) * score_scale
            scores = jnp.where(allowed[:, None, :], scores, -jnp.inf)
            peak_row = lax.optimization_barrier(jnp.max(scores, axis=-1)).astype(jnp.bfloat16)
            weights = jnp.exp(scores - peak_row.astype(jnp.float32)[..., None])
            total_row = lax.optimization_barrier(jnp.sum(weights, axis=-1)).astype(jnp.bfloat16)
            rounded = weights.astype(jnp.bfloat16).astype(jnp.float32)
            mixed = jnp.einsum('rgk,kd->rgd', rounded, values_taken)
            head_outputs.append((mixed / total_row.astype(jnp.float32)[..., None]).astype(jnp.bfloat16))
            head_peaks.append(peak_row)
            head_totals.append(total_row)
        return (jnp.stack(head_outputs, 1), jnp.stack(head_peaks, 1), jnp.stack(head_totals, 1))
    block_ids = jnp.arange(picked.shape[0], dtype=jnp.int32)
    outputs, peaks, totals = lax.map(one_block, (block_ids, picked, usable))
    heads_all = head_count * group_size
    return (outputs.reshape(query_tokens, heads_all, HD), peaks.reshape(query_tokens, heads_all), totals.reshape(query_tokens, heads_all))

def combine_pair(first, second):
    peak_first, total_first, acc_first = first
    peak_second, total_second, acc_second = second
    peak_joint = jnp.maximum(peak_first, peak_second)
    factor_first = jnp.exp(peak_first - peak_joint)
    factor_second = jnp.exp(peak_second - peak_joint)
    total_joint = total_first * factor_first + total_second * factor_second
    acc_joint = acc_first * factor_first[..., None] + acc_second * factor_second[..., None]
    return (peak_joint, total_joint, acc_joint)

def reference(queries, key_cache, value_cache, blocks, out_weight):

    def advance(carry, shard_index):
        key_shard = lax.dynamic_slice_in_dim(key_cache, shard_index * CTX_DEV, CTX_DEV, 0)
        value_shard = lax.dynamic_slice_in_dim(value_cache, shard_index * CTX_DEV, CTX_DEV, 0)
        outputs, peaks, totals = shard_partials(queries, key_shard, value_shard, blocks, shard_index * BPS, CTX, KVH)
        totals_wide = totals.astype(jnp.float32)
        states_now = (peaks.astype(jnp.float32), totals_wide, outputs.astype(jnp.float32) * totals_wide[..., None])
        return (combine_pair(carry, states_now), None)
    start_state = (jnp.full((QTOK, HQ), -jnp.inf, jnp.float32), jnp.zeros((QTOK, HQ), jnp.float32), jnp.zeros((QTOK, HQ, HD), jnp.float32))
    final_state, unused = lax.scan(advance, start_state, jnp.arange(N_CTX, dtype=jnp.int32))
    attended_heads = (final_state[2] / final_state[1][..., None]).astype(jnp.bfloat16).reshape(QTOK, HQ * HD)
    return jnp.dot(attended_heads, out_weight, preferred_element_type=jnp.float32).astype(jnp.bfloat16)
```

```python
import functools
import math

import jax
import jax.numpy as jnp
from jax import lax
from jax.experimental import pallas as pl
from jax.experimental.pallas import tpu as pltpu
from jax.sharding import PartitionSpec as P

HD = 128
BLK = 128
MOST = 7


def block_tables(block_lists, shard_first, blocks_here):
    below = jnp.sum((block_lists < shard_first).astype(jnp.int32), axis=-1)
    inside = jnp.sum(
        ((block_lists >= shard_first) & (block_lists < shard_first + blocks_here)).astype(
            jnp.int32
        ),
        axis=-1,
    )
    slot_ids = jnp.arange(MOST, dtype=jnp.int32)
    places = jnp.clip(below[..., None] + slot_ids, 0, block_lists.shape[-1] - 1)
    picked = jnp.take_along_axis(block_lists, places, axis=-1) - shard_first
    usable = slot_ids < inside[..., None]
    picked = jnp.where(usable, picked, 0)
    return picked, inside


def attn_kernel(picked_ref, count_ref, pos_ref, q_ref, k_ref, v_ref, part_ref, stat_ref, sc_ref,
                *, heads, rows, tq, score_scale):
    h = pl.program_id(0)
    b = pl.program_id(1)
    item = b * heads + h
    n = count_ref[item]
    q = q_ref[...].reshape(rows, HD)
    key_ids = lax.broadcasted_iota(jnp.int32, (BLK, rows), 0)
    row_ids = lax.broadcasted_iota(jnp.int32, (BLK, rows), 1)
    tok = (row_ids // (rows // (BLK // tq))) * tq + row_ids % tq
    limit = b * BLK + tok - pos_ref[0]

    def first(s, m):
        blk = picked_ref[item * MOST + s]
        start = pl.multiple_of(blk * BLK, BLK)
        kb = k_ref[pl.ds(start, BLK), :]
        sc = lax.dot_general(kb, q, (((1,), (1,)), ((), ())), preferred_element_type=jnp.float32)
        sc = sc * score_scale
        sc = jnp.where(blk * BLK + key_ids <= limit, sc, -jnp.inf)
        sc_ref[s] = sc
        return jnp.maximum(m, jnp.max(sc, axis=0, keepdims=True))

    m = lax.fori_loop(0, n, first, jnp.full((1, rows), -jnp.inf, jnp.float32))
    peak = m.astype(jnp.bfloat16).astype(jnp.float32)

    def second(s, carry):
        tot, acc = carry
        blk = picked_ref[item * MOST + s]
        start = pl.multiple_of(blk * BLK, BLK)
        vb = v_ref[pl.ds(start, BLK), :]
        w = jnp.exp(sc_ref[s] - peak)
        tot = tot + jnp.sum(w, axis=0, keepdims=True)
        acc = acc + lax.dot_general(
            vb, w.astype(jnp.bfloat16), (((0,), (0,)), ((), ())),
            preferred_element_type=jnp.float32,
        )
        return tot, acc

    tot, acc = lax.fori_loop(
        0, n, second,
        (jnp.zeros((1, rows), jnp.float32), jnp.zeros((HD, rows), jnp.float32)),
    )
    total = tot.astype(jnp.bfloat16).astype(jnp.float32)
    out = (acc / total).astype(jnp.bfloat16)
    chunks = part_ref.shape[1]
    width = rows // chunks
    for j in range(chunks):
        part_ref[0, j, 0] = out[:, j * width:(j + 1) * width]
    stat_ref[0, 0, 0:1, :] = peak
    stat_ref[0, 0, 1:2, :] = total


def on_device(queries, key_cache, value_cache, blocks, out_weight):
    shard_count = lax.axis_size("ctx")
    here_index = lax.axis_index("ctx")
    local_heads = key_cache.shape[1] // HD
    tq = queries.shape[0]
    group_size = queries.shape[1] // (local_heads * HD)
    blocks_here = key_cache.shape[0] // BLK
    query_tokens = tq * shard_count
    qblocks = query_tokens // BLK
    per_block = shard_count // qblocks
    rows = group_size * BLK
    total_keys = shard_count * key_cache.shape[0]

    block_lists = lax.dynamic_slice_in_dim(
        blocks, lax.axis_index("kv") * local_heads, local_heads, 1
    )
    shard_first = here_index * blocks_here
    picked, inside = block_tables(block_lists, shard_first, blocks_here)
    pos0 = (shard_first * BLK - (total_keys - query_tokens)).astype(jnp.int32).reshape(1)

    qt = queries.reshape(tq, local_heads * group_size, HD).transpose(1, 0, 2)
    q_all = lax.all_gather(qt, "ctx", axis=0, tiled=False)
    q_all = q_all.reshape(qblocks, per_block, local_heads, group_size, tq, HD)

    kernel = functools.partial(
        attn_kernel, heads=local_heads, rows=rows, tq=tq, score_scale=1.0 / math.sqrt(HD)
    )
    grid_spec = pltpu.PrefetchScalarGridSpec(
        num_scalar_prefetch=3,
        grid=(local_heads, qblocks),
        in_specs=[
            pl.BlockSpec((1, per_block, 1, group_size, tq, HD),
                         lambda h, b, *_: (b, 0, h, 0, 0, 0)),
            pl.BlockSpec((key_cache.shape[0], HD), lambda h, b, *_: (0, h)),
            pl.BlockSpec((value_cache.shape[0], HD), lambda h, b, *_: (0, h)),
        ],
        out_specs=[
            pl.BlockSpec((1, per_block, 1, HD, rows // per_block),
                         lambda h, b, *_: (b, 0, h, 0, 0)),
            pl.BlockSpec((1, 1, 2, rows), lambda h, b, *_: (b, h, 0, 0)),
        ],
        scratch_shapes=[pltpu.VMEM((MOST, BLK, rows), jnp.float32)],
    )
    part, stat = pl.pallas_call(
        kernel,
        grid_spec=grid_spec,
        out_shape=[
            jax.ShapeDtypeStruct((qblocks, per_block, local_heads, HD, rows // per_block),
                                 jnp.bfloat16),
            jax.ShapeDtypeStruct((qblocks, local_heads, 2, rows), jnp.float32),
        ],
        compiler_params=pltpu.CompilerParams(
            dimension_semantics=("arbitrary", "arbitrary"),
        ),
    )(picked.reshape(-1).astype(jnp.int32), inside.reshape(-1).astype(jnp.int32), pos0,
      q_all, key_cache, value_cache)

    width = rows // per_block
    part = part.reshape(shard_count, local_heads, HD, width)
    stat = stat.reshape(qblocks, local_heads, 2, per_block, width).transpose(0, 3, 1, 2, 4)
    stat = stat.reshape(shard_count, local_heads, 2, width).astype(jnp.bfloat16)
    part_in = lax.all_to_all(part, "ctx", 0, 0, tiled=True)
    stat_in = lax.all_to_all(stat, "ctx", 0, 0, tiled=True).astype(jnp.float32)

    peak_all = stat_in[:, :, 0, :]
    peak_top = jnp.max(peak_all, axis=0)
    weight_all = stat_in[:, :, 1, :] * jnp.exp(peak_all - peak_top)
    summed = jnp.sum(weight_all[:, :, None, :] * part_in.astype(jnp.float32), axis=0)
    merged = summed / jnp.sum(weight_all, axis=0)[:, None, :]
    merged = merged.reshape(local_heads, HD, group_size, tq).transpose(3, 0, 2, 1)
    attended_heads = merged.astype(jnp.bfloat16).reshape(tq, -1)
    projected = jnp.dot(
        lax.all_gather(attended_heads, "ctx", axis=0, tiled=True),
        out_weight,
        preferred_element_type=jnp.float32,
    )
    return lax.psum_scatter(projected.astype(jnp.bfloat16), "kv", scatter_dimension=0, tiled=True)


def solution(mesh):
    placed = (P("ctx", "kv"), P("ctx", "kv"), P("ctx", "kv"), P(), P("kv", "ctx"))
    return jax.shard_map(
        on_device, mesh=mesh, in_specs=placed, out_specs=P("kv", "ctx"), check_vma=False
    )
```

```python
import functools
import math

import jax
import jax.numpy as jnp
from jax import lax
from jax.experimental import pallas as pl
from jax.experimental.pallas import tpu as pltpu
from jax.sharding import PartitionSpec as P

HD = 128
BLK = 128
MOST = 7


def block_tables(block_lists, shard_first, blocks_here):
    below = jnp.sum((block_lists < shard_first).astype(jnp.int32), axis=-1)
    inside = jnp.sum(
        ((block_lists >= shard_first) & (block_lists < shard_first + blocks_here)).astype(
            jnp.int32
        ),
        axis=-1,
    )
    slot_ids = jnp.arange(MOST, dtype=jnp.int32)
    places = jnp.clip(below[..., None] + slot_ids, 0, block_lists.shape[-1] - 1)
    picked = jnp.take_along_axis(block_lists, places, axis=-1) - shard_first
    usable = slot_ids < inside[..., None]
    picked = jnp.where(usable, picked, 0)
    return picked, inside


def attn_kernel(picked_ref, count_ref, pos_ref, q_ref, k_ref, v_ref, part_ref, sc_ref,
                *, rows, tq, score_scale):
    b = pl.program_id(0)
    n = count_ref[b]
    q = q_ref[...].reshape(rows, HD)
    key_ids = lax.broadcasted_iota(jnp.int32, (BLK, rows), 0)
    row_ids = lax.broadcasted_iota(jnp.int32, (BLK, rows), 1)
    tok = (row_ids // (rows // (BLK // tq))) * tq + row_ids % tq
    limit = b * BLK + tok - pos_ref[0]

    def first(s, m):
        blk = picked_ref[b * MOST + s]
        start = pl.multiple_of(blk * BLK, BLK)
        kb = k_ref[pl.ds(start, BLK), :]
        sc = lax.dot_general(kb, q, (((1,), (1,)), ((), ())), preferred_element_type=jnp.float32)
        sc = sc * score_scale
        sc = jnp.where(blk * BLK + key_ids <= limit, sc, -jnp.inf)
        sc_ref[s] = sc
        return jnp.maximum(m, jnp.max(sc, axis=0, keepdims=True))

    m = lax.fori_loop(0, n, first, jnp.full((1, rows), -jnp.inf, jnp.float32))
    peak = m.astype(jnp.bfloat16).astype(jnp.float32)

    def second(s, carry):
        tot, acc = carry
        blk = picked_ref[b * MOST + s]
        start = pl.multiple_of(blk * BLK, BLK)
        vb = v_ref[pl.ds(start, BLK), :]
        w = jnp.exp(sc_ref[s] - peak)
        tot = tot + jnp.sum(w, axis=0, keepdims=True)
        acc = acc + lax.dot_general(
            vb, w.astype(jnp.bfloat16), (((0,), (0,)), ((), ())),
            preferred_element_type=jnp.float32,
        )
        return tot, acc

    tot, acc = lax.fori_loop(
        0, n, second,
        (jnp.zeros((1, rows), jnp.float32), jnp.zeros((HD, rows), jnp.float32)),
    )
    total = tot.astype(jnp.bfloat16).astype(jnp.float32)
    out = (acc / total).astype(jnp.bfloat16)
    extra = part_ref.shape[2] - HD
    slab_rows = lax.broadcasted_iota(jnp.int32, (extra, rows), 0)
    slab = jnp.where(slab_rows == 0, peak, jnp.where(slab_rows == 1, total, 0.0))
    slab = slab.astype(jnp.bfloat16)
    chunks = part_ref.shape[1]
    width = rows // chunks
    for j in range(chunks):
        part_ref[0, j, 0:HD, :] = out[:, j * width:(j + 1) * width]
        part_ref[0, j, HD:, :] = slab[:, j * width:(j + 1) * width]


def head_stream(head, q_h, key_cache, value_cache, picked, inside, pos0, shard_count, before):
    qblocks, per_block, group_size, tq = q_h.shape[:4]
    rows = group_size * BLK
    width = rows // per_block
    extra = 16
    kernel = functools.partial(
        attn_kernel, rows=rows, tq=tq, score_scale=1.0 / math.sqrt(HD)
    )
    grid_spec = pltpu.PrefetchScalarGridSpec(
        num_scalar_prefetch=3,
        grid=(qblocks,),
        in_specs=[
            pl.BlockSpec((1, per_block, group_size, tq, HD), lambda b, *_: (b, 0, 0, 0, 0)),
            pl.BlockSpec((key_cache.shape[0], HD), lambda b, *_: (0, head)),
            pl.BlockSpec((value_cache.shape[0], HD), lambda b, *_: (0, head)),
        ],
        out_specs=pl.BlockSpec((1, per_block, HD + extra, width), lambda b, *_: (b, 0, 0, 0)),
        scratch_shapes=[pltpu.VMEM((MOST, BLK, rows), jnp.float32)],
    )
    part = pl.pallas_call(
        kernel,
        grid_spec=grid_spec,
        out_shape=jax.ShapeDtypeStruct((qblocks, per_block, HD + extra, width), jnp.bfloat16),
        compiler_params=pltpu.CompilerParams(dimension_semantics=("arbitrary",)),
    )(picked[:, head].reshape(-1).astype(jnp.int32), inside[:, head].astype(jnp.int32), pos0,
      q_h, key_cache, value_cache)

    part = part.reshape(shard_count, HD + extra, width)
    if before is not None:
        part, before = lax.optimization_barrier((part, before))
    part_in = lax.all_to_all(part, "ctx", 0, 0, tiled=True)
    part_in = part_in.astype(jnp.float32)
    peak_all = part_in[:, HD, :]
    peak_top = jnp.max(peak_all, axis=0)
    weight_all = part_in[:, HD + 1, :] * jnp.exp(peak_all - peak_top)
    summed = jnp.sum(weight_all[:, None, :] * part_in[:, :HD, :], axis=0)
    merged = summed / jnp.sum(weight_all, axis=0)[None, :]
    merged = merged.reshape(HD, group_size, tq).transpose(2, 1, 0)
    return merged.astype(jnp.bfloat16).reshape(tq, group_size * HD), before


def on_device(queries, key_cache, value_cache, blocks, out_weight):
    shard_count = lax.axis_size("ctx")
    here_index = lax.axis_index("ctx")
    local_heads = key_cache.shape[1] // HD
    tq = queries.shape[0]
    group_size = queries.shape[1] // (local_heads * HD)
    blocks_here = key_cache.shape[0] // BLK
    query_tokens = tq * shard_count
    qblocks = query_tokens // BLK
    per_block = shard_count // qblocks
    total_keys = shard_count * key_cache.shape[0]

    block_lists = lax.dynamic_slice_in_dim(
        blocks, lax.axis_index("kv") * local_heads, local_heads, 1
    )
    shard_first = here_index * blocks_here
    picked, inside = block_tables(block_lists, shard_first, blocks_here)
    pos0 = (shard_first * BLK - (total_keys - query_tokens)).astype(jnp.int32).reshape(1)

    qt = queries.reshape(tq, local_heads, group_size, HD).transpose(1, 2, 0, 3)
    attended = []
    for head in range(local_heads):
        q_h = lax.all_gather(qt[head], "ctx", axis=0, tiled=False)
        q_h = q_h.reshape(qblocks, per_block, group_size, tq, HD)
        attended_h, earlier = head_stream(
            head, q_h, key_cache, value_cache, picked, inside, pos0, shard_count,
            attended[-1] if attended else None,
        )
        if earlier is not None:
            attended[-1] = earlier
        attended.append(attended_h)
    rows_w = group_size * HD
    projected = None
    for head in range(local_heads):
        term = jnp.dot(
            lax.all_gather(attended[head], "ctx", axis=0, tiled=True),
            out_weight[head * rows_w:(head + 1) * rows_w],
            preferred_element_type=jnp.float32,
        )
        projected = term if projected is None else projected + term
    return lax.psum_scatter(projected.astype(jnp.bfloat16), "kv", scatter_dimension=0, tiled=True)


def solution(mesh):
    placed = (P("ctx", "kv"), P("ctx", "kv"), P("ctx", "kv"), P(), P("kv", "ctx"))
    return jax.shard_map(
        on_device, mesh=mesh, in_specs=placed, out_specs=P("kv", "ctx"), check_vma=False
    )
```

```python
import functools
import math

import jax
import jax.numpy as jnp
from jax import lax
from jax.experimental import pallas as pl
from jax.experimental.pallas import tpu as pltpu
from jax.sharding import PartitionSpec as P

HD = 128
BLK = 128
MOST = 7


def block_tables(block_lists, shard_first, blocks_here):
    below = jnp.sum((block_lists < shard_first).astype(jnp.int32), axis=-1)
    inside = jnp.sum(
        ((block_lists >= shard_first) & (block_lists < shard_first + blocks_here)).astype(
            jnp.int32
        ),
        axis=-1,
    )
    slot_ids = jnp.arange(MOST, dtype=jnp.int32)
    places = jnp.clip(below[..., None] + slot_ids, 0, block_lists.shape[-1] - 1)
    picked = jnp.take_along_axis(block_lists, places, axis=-1) - shard_first
    usable = slot_ids < inside[..., None]
    picked = jnp.where(usable, picked, 0)
    return picked, inside


def attn_kernel(picked_ref, count_ref, pos_ref, q_ref, k_ref, v_ref, part_ref, sc_ref,
                *, heads, rows, tq, score_scale):
    h = pl.program_id(0)
    b = pl.program_id(1)
    item = b * heads + h
    n = count_ref[item]
    q = q_ref[...].reshape(rows, HD)
    key_ids = lax.broadcasted_iota(jnp.int32, (BLK, rows), 0)
    row_ids = lax.broadcasted_iota(jnp.int32, (BLK, rows), 1)
    tok = (row_ids // (rows // (BLK // tq))) * tq + row_ids % tq
    limit = b * BLK + tok - pos_ref[0]

    def first(s, m):
        blk = picked_ref[item * MOST + s]
        start = pl.multiple_of(blk * BLK, BLK)
        kb = k_ref[pl.ds(start, BLK), :]
        sc = lax.dot_general(kb, q, (((1,), (1,)), ((), ())), preferred_element_type=jnp.float32)
        sc = sc * score_scale
        sc = jnp.where(blk * BLK + key_ids <= limit, sc, -jnp.inf)
        sc_ref[s] = sc
        return jnp.maximum(m, jnp.max(sc, axis=0, keepdims=True))

    m = lax.fori_loop(0, n, first, jnp.full((1, rows), -jnp.inf, jnp.float32))
    peak = m.astype(jnp.bfloat16).astype(jnp.float32)

    def second(s, carry):
        tot, acc = carry
        blk = picked_ref[item * MOST + s]
        start = pl.multiple_of(blk * BLK, BLK)
        vb = v_ref[pl.ds(start, BLK), :]
        w = jnp.exp(sc_ref[s] - peak)
        tot = tot + jnp.sum(w, axis=0, keepdims=True)
        acc = acc + lax.dot_general(
            vb, w.astype(jnp.bfloat16), (((0,), (0,)), ((), ())),
            preferred_element_type=jnp.float32,
        )
        return tot, acc

    tot, acc = lax.fori_loop(
        0, n, second,
        (jnp.zeros((1, rows), jnp.float32), jnp.zeros((HD, rows), jnp.float32)),
    )
    total = tot.astype(jnp.bfloat16).astype(jnp.float32)
    out = (acc / total).astype(jnp.bfloat16)
    extra = part_ref.shape[3] - HD
    slab_rows = lax.broadcasted_iota(jnp.int32, (extra, rows), 0)
    slab = jnp.where(slab_rows == 0, peak, jnp.where(slab_rows == 1, total, 0.0))
    slab = slab.astype(jnp.bfloat16)
    chunks = part_ref.shape[1]
    width = rows // chunks
    for j in range(chunks):
        part_ref[0, j, 0, 0:HD, :] = out[:, j * width:(j + 1) * width]
        part_ref[0, j, 0, HD:, :] = slab[:, j * width:(j + 1) * width]


def on_device(queries, key_cache, value_cache, blocks, out_weight):
    shard_count = lax.axis_size("ctx")
    here_index = lax.axis_index("ctx")
    local_heads = key_cache.shape[1] // HD
    tq = queries.shape[0]
    group_size = queries.shape[1] // (local_heads * HD)
    blocks_here = key_cache.shape[0] // BLK
    query_tokens = tq * shard_count
    qblocks = query_tokens // BLK
    per_block = shard_count // qblocks
    rows = group_size * BLK
    width = rows // per_block
    extra = 16
    total_keys = shard_count * key_cache.shape[0]

    block_lists = lax.dynamic_slice_in_dim(
        blocks, lax.axis_index("kv") * local_heads, local_heads, 1
    )
    shard_first = here_index * blocks_here
    picked, inside = block_tables(block_lists, shard_first, blocks_here)
    pos0 = (shard_first * BLK - (total_keys - query_tokens)).astype(jnp.int32).reshape(1)

    qt = queries.reshape(tq, local_heads * group_size, HD).transpose(1, 0, 2)
    q_all = lax.all_gather(qt, "ctx", axis=0, tiled=False)
    q_all = q_all.reshape(qblocks, per_block, local_heads, group_size, tq, HD)

    kernel = functools.partial(
        attn_kernel, heads=local_heads, rows=rows, tq=tq, score_scale=1.0 / math.sqrt(HD)
    )
    grid_spec = pltpu.PrefetchScalarGridSpec(
        num_scalar_prefetch=3,
        grid=(local_heads, qblocks),
        in_specs=[
            pl.BlockSpec((1, per_block, 1, group_size, tq, HD),
                         lambda h, b, *_: (b, 0, h, 0, 0, 0)),
            pl.BlockSpec((key_cache.shape[0], HD), lambda h, b, *_: (0, h)),
            pl.BlockSpec((value_cache.shape[0], HD), lambda h, b, *_: (0, h)),
        ],
        out_specs=pl.BlockSpec((1, per_block, 1, HD + extra, width),
                               lambda h, b, *_: (b, 0, h, 0, 0)),
        scratch_shapes=[pltpu.VMEM((MOST, BLK, rows), jnp.float32)],
    )
    part = pl.pallas_call(
        kernel,
        grid_spec=grid_spec,
        out_shape=jax.ShapeDtypeStruct(
            (qblocks, per_block, local_heads, HD + extra, width), jnp.bfloat16
        ),
        compiler_params=pltpu.CompilerParams(
            dimension_semantics=("arbitrary", "arbitrary"),
        ),
    )(picked.reshape(-1).astype(jnp.int32), inside.reshape(-1).astype(jnp.int32), pos0,
      q_all, key_cache, value_cache)

    part = part.reshape(shard_count, local_heads, HD + extra, width)
    part_in = lax.all_to_all(part, "ctx", 0, 0, tiled=True).astype(jnp.float32)
    peak_all = part_in[:, :, HD, :]
    peak_top = jnp.max(peak_all, axis=0)
    weight_all = part_in[:, :, HD + 1, :] * jnp.exp(peak_all - peak_top)
    summed = jnp.sum(weight_all[:, :, None, :] * part_in[:, :, :HD, :], axis=0)
    merged = summed / jnp.sum(weight_all, axis=0)[:, None, :]
    merged = merged.reshape(local_heads, HD, group_size, tq).transpose(3, 0, 2, 1)
    attended_heads = merged.astype(jnp.bfloat16).reshape(tq, -1)
    projected = jnp.dot(
        lax.all_gather(attended_heads, "ctx", axis=0, tiled=True),
        out_weight,
        preferred_element_type=jnp.float32,
    )
    return lax.psum_scatter(projected.astype(jnp.bfloat16), "kv", scatter_dimension=0, tiled=True)


def solution(mesh):
    placed = (P("ctx", "kv"), P("ctx", "kv"), P("ctx", "kv"), P(), P("kv", "ctx"))
    return jax.shard_map(
        on_device, mesh=mesh, in_specs=placed, out_specs=P("kv", "ctx"), check_vma=False
    )
```

```python
import functools
import math

import jax
import jax.numpy as jnp
from jax import lax
from jax.experimental import pallas as pl
from jax.experimental.pallas import tpu as pltpu
from jax.sharding import PartitionSpec as P

HD = 128
BLK = 128
MOST = 7


def block_tables(block_lists, shard_first, blocks_here):
    below = jnp.sum((block_lists < shard_first).astype(jnp.int32), axis=-1)
    inside = jnp.sum(
        ((block_lists >= shard_first) & (block_lists < shard_first + blocks_here)).astype(
            jnp.int32
        ),
        axis=-1,
    )
    slot_ids = jnp.arange(MOST, dtype=jnp.int32)
    places = jnp.clip(below[..., None] + slot_ids, 0, block_lists.shape[-1] - 1)
    picked = jnp.take_along_axis(block_lists, places, axis=-1) - shard_first
    usable = slot_ids < inside[..., None]
    picked = jnp.where(usable, picked, 0)
    return picked, inside


def attn_kernel(picked_ref, count_ref, pos_ref, q_ref, k_ref, v_ref, part_ref, sc_ref,
                *, heads, rows, tq, score_scale):
    h = pl.program_id(0)
    b = pl.program_id(1)
    item = b * heads + h
    n = count_ref[item]
    q = q_ref[...].reshape(rows, HD)
    first_query = b * BLK - pos_ref[0]

    def masked(sc, blk):
        key_ids = lax.broadcasted_iota(jnp.int32, (BLK, rows), 0)
        row_ids = lax.broadcasted_iota(jnp.int32, (BLK, rows), 1)
        tok = (row_ids // (rows // (BLK // tq))) * tq + row_ids % tq
        return jnp.where(blk * BLK + key_ids <= first_query + tok, sc, -jnp.inf)

    def first(s, m):
        blk = picked_ref[item * MOST + s]
        start = pl.multiple_of(blk * BLK, BLK)
        kb = k_ref[pl.ds(start, BLK), :]
        sc = lax.dot_general(kb, q, (((1,), (1,)), ((), ())), preferred_element_type=jnp.float32)
        sc = sc * score_scale
        sc = lax.cond(blk * BLK + BLK - 1 > first_query, masked, lambda x, y: x, sc, blk)
        sc_ref[s] = sc
        return jnp.maximum(m, jnp.max(sc, axis=0, keepdims=True))

    m = lax.fori_loop(0, n, first, jnp.full((1, rows), -jnp.inf, jnp.float32))
    peak = m.astype(jnp.bfloat16).astype(jnp.float32)

    def second(s, acc):
        blk = picked_ref[item * MOST + s]
        start = pl.multiple_of(blk * BLK, BLK)
        vb = v_ref[0, :, pl.ds(start, BLK)]
        w = jnp.exp(sc_ref[s] - peak).astype(jnp.bfloat16)
        return acc + jnp.dot(vb, w, preferred_element_type=jnp.float32)

    acc = lax.fori_loop(0, n, second, jnp.zeros((v_ref.shape[1], rows), jnp.float32))
    total = acc[HD:HD + 1].astype(jnp.bfloat16).astype(jnp.float32)
    out = (acc[:HD] / total).astype(jnp.bfloat16)
    extra = part_ref.shape[3] - HD
    slab_rows = lax.broadcasted_iota(jnp.int32, (extra, rows), 0)
    slab = jnp.where(slab_rows == 0, peak, jnp.where(slab_rows == 1, total, 0.0))
    slab = slab.astype(jnp.bfloat16)
    chunks = part_ref.shape[1]
    width = rows // chunks
    for j in range(chunks):
        part_ref[0, j, 0, 0:HD, :] = out[:, j * width:(j + 1) * width]
        part_ref[0, j, 0, HD:, :] = slab[:, j * width:(j + 1) * width]


def on_device(queries, key_cache, value_cache, blocks, out_weight):
    shard_count = lax.axis_size("ctx")
    here_index = lax.axis_index("ctx")
    local_heads = key_cache.shape[1] // HD
    tq = queries.shape[0]
    group_size = queries.shape[1] // (local_heads * HD)
    blocks_here = key_cache.shape[0] // BLK
    query_tokens = tq * shard_count
    qblocks = query_tokens // BLK
    per_block = shard_count // qblocks
    rows = group_size * BLK
    width = rows // per_block
    extra = 16
    total_keys = shard_count * key_cache.shape[0]

    block_lists = lax.dynamic_slice_in_dim(
        blocks, lax.axis_index("kv") * local_heads, local_heads, 1
    )
    shard_first = here_index * blocks_here
    picked, inside = block_tables(block_lists, shard_first, blocks_here)
    pos0 = (shard_first * BLK - (total_keys - query_tokens)).astype(jnp.int32).reshape(1)

    values_t = value_cache.reshape(value_cache.shape[0], local_heads, HD).transpose(1, 2, 0)
    values_t = jnp.concatenate(
        [values_t, jnp.ones((local_heads, extra, value_cache.shape[0]), jnp.bfloat16)], axis=1
    )
    qt = queries.reshape(tq, local_heads * group_size, HD).transpose(1, 0, 2)
    q_all = lax.all_gather(qt, "ctx", axis=0, tiled=False)
    q_all = q_all.reshape(qblocks, per_block, local_heads, group_size, tq, HD)

    kernel = functools.partial(
        attn_kernel, heads=local_heads, rows=rows, tq=tq, score_scale=1.0 / math.sqrt(HD)
    )
    grid_spec = pltpu.PrefetchScalarGridSpec(
        num_scalar_prefetch=3,
        grid=(local_heads, qblocks),
        in_specs=[
            pl.BlockSpec((1, per_block, 1, group_size, tq, HD),
                         lambda h, b, *_: (b, 0, h, 0, 0, 0)),
            pl.BlockSpec((key_cache.shape[0], HD), lambda h, b, *_: (0, h)),
            pl.BlockSpec((1, HD + extra, value_cache.shape[0]), lambda h, b, *_: (h, 0, 0)),
        ],
        out_specs=pl.BlockSpec((1, per_block, 1, HD + extra, width),
                               lambda h, b, *_: (b, 0, h, 0, 0)),
        scratch_shapes=[pltpu.VMEM((MOST, BLK, rows), jnp.float32)],
    )
    part = pl.pallas_call(
        kernel,
        grid_spec=grid_spec,
        out_shape=jax.ShapeDtypeStruct(
            (qblocks, per_block, local_heads, HD + extra, width), jnp.bfloat16
        ),
        compiler_params=pltpu.CompilerParams(
            dimension_semantics=("arbitrary", "arbitrary"),
        ),
    )(picked.reshape(-1).astype(jnp.int32), inside.reshape(-1).astype(jnp.int32), pos0,
      q_all, key_cache, values_t)

    part = part.reshape(shard_count, local_heads, HD + extra, width)
    part_in = lax.all_to_all(part, "ctx", 0, 0, tiled=True).astype(jnp.float32)
    peak_all = part_in[:, :, HD, :]
    peak_top = jnp.max(peak_all, axis=0)
    weight_all = part_in[:, :, HD + 1, :] * jnp.exp(peak_all - peak_top)
    summed = jnp.sum(weight_all[:, :, None, :] * part_in[:, :, :HD, :], axis=0)
    merged = summed / jnp.sum(weight_all, axis=0)[:, None, :]
    merged = merged.reshape(local_heads, HD, group_size, tq).transpose(3, 0, 2, 1)
    attended_heads = merged.astype(jnp.bfloat16).reshape(tq, -1)
    projected = jnp.dot(
        lax.all_gather(attended_heads, "ctx", axis=0, tiled=True),
        out_weight,
        preferred_element_type=jnp.float32,
    )
    return lax.psum_scatter(projected.astype(jnp.bfloat16), "kv", scatter_dimension=0, tiled=True)


def solution(mesh):
    placed = (P("ctx", "kv"), P("ctx", "kv"), P("ctx", "kv"), P(), P("kv", "ctx"))
    return jax.shard_map(
        on_device, mesh=mesh, in_specs=placed, out_specs=P("kv", "ctx"), check_vma=False
    )
```

```python
import functools
import math

import jax
import jax.numpy as jnp
from jax import lax
from jax.experimental import pallas as pl
from jax.experimental.pallas import tpu as pltpu
from jax.sharding import PartitionSpec as P

HD = 128
BLK = 128
MOST = 7

ORDERS = ((8, 4, 32, 16, 2), (32, 8, 4, 2, 16))


def gather_ctx(x):
    n = lax.axis_size("ctx")
    me = lax.axis_index("ctx")
    core = me % 2
    steps = len(ORDERS[0])
    buf = x[None]
    for step in range(steps):
        a0, a1 = ORDERS[0][step], ORDERS[1][step]
        pairs = [(c, c ^ (a0 if c % 2 == 0 else a1)) for c in range(n)]
        other = lax.ppermute(buf, "ctx", pairs)
        low = (me & jnp.where(core == 0, a0, a1)) == 0
        buf = jnp.where(low, jnp.concatenate([buf, other]), jnp.concatenate([other, buf]))
    tail = buf.shape[1:]
    outs = []
    for order in ORDERS:
        dims_bits = [order[steps - 1 - d].bit_length() - 2 for d in range(steps)]
        perm = [dims_bits.index(bb) for bb in reversed(range(steps))]
        t = buf.reshape((2,) * steps + tail)
        t = t.transpose(perm + list(range(steps, steps + len(tail))))
        outs.append(t.reshape((2 ** steps,) + tail))
    mine = jnp.where(core == 0, outs[0], outs[1])
    other = lax.ppermute(mine, "ctx", [(c, c ^ 1) for c in range(n)])
    both = jnp.where(core == 0, jnp.stack([mine, other], 1), jnp.stack([other, mine], 1))
    return both.reshape((n,) + tail)


def block_tables(block_lists, shard_first, blocks_here):
    below = jnp.sum((block_lists < shard_first).astype(jnp.int32), axis=-1)
    inside = jnp.sum(
        ((block_lists >= shard_first) & (block_lists < shard_first + blocks_here)).astype(
            jnp.int32
        ),
        axis=-1,
    )
    slot_ids = jnp.arange(MOST, dtype=jnp.int32)
    places = jnp.clip(below[..., None] + slot_ids, 0, block_lists.shape[-1] - 1)
    picked = jnp.take_along_axis(block_lists, places, axis=-1) - shard_first
    usable = slot_ids < inside[..., None]
    picked = jnp.where(usable, picked, 0)
    return picked, inside


def attn_kernel(picked_ref, count_ref, pos_ref, q_ref, k_ref, v_ref, part_ref, sc_ref,
                *, heads, rows, tq, score_scale):
    h = pl.program_id(0)
    b = pl.program_id(1)
    item = b * heads + h
    n = count_ref[item]
    q = q_ref[...].reshape(rows, HD)
    key_ids = lax.broadcasted_iota(jnp.int32, (BLK, rows), 0)
    row_ids = lax.broadcasted_iota(jnp.int32, (BLK, rows), 1)
    tok = (row_ids // (rows // (BLK // tq))) * tq + row_ids % tq
    limit = b * BLK + tok - pos_ref[0]

    def first(s, m):
        blk = picked_ref[item * MOST + s]
        start = pl.multiple_of(blk * BLK, BLK)
        kb = k_ref[pl.ds(start, BLK), :]
        sc = lax.dot_general(kb, q, (((1,), (1,)), ((), ())), preferred_element_type=jnp.float32)
        sc = sc * score_scale
        sc = jnp.where(blk * BLK + key_ids <= limit, sc, -jnp.inf)
        sc_ref[s] = sc
        return jnp.maximum(m, jnp.max(sc, axis=0, keepdims=True))

    m = lax.fori_loop(0, n, first, jnp.full((1, rows), -jnp.inf, jnp.float32))
    peak = m.astype(jnp.bfloat16).astype(jnp.float32)

    def second(s, carry):
        tot, acc = carry
        blk = picked_ref[item * MOST + s]
        start = pl.multiple_of(blk * BLK, BLK)
        vb = v_ref[pl.ds(start, BLK), :]
        w = jnp.exp(sc_ref[s] - peak)
        tot = tot + jnp.sum(w, axis=0, keepdims=True)
        acc = acc + lax.dot_general(
            vb, w.astype(jnp.bfloat16), (((0,), (0,)), ((), ())),
            preferred_element_type=jnp.float32,
        )
        return tot, acc

    tot, acc = lax.fori_loop(
        0, n, second,
        (jnp.zeros((1, rows), jnp.float32), jnp.zeros((HD, rows), jnp.float32)),
    )
    total = tot.astype(jnp.bfloat16).astype(jnp.float32)
    out = (acc / total).astype(jnp.bfloat16)
    extra = part_ref.shape[3] - HD
    slab_rows = lax.broadcasted_iota(jnp.int32, (extra, rows), 0)
    slab = jnp.where(slab_rows == 0, peak, jnp.where(slab_rows == 1, total, 0.0))
    slab = slab.astype(jnp.bfloat16)
    chunks = part_ref.shape[1]
    width = rows // chunks
    for j in range(chunks):
        part_ref[0, j, 0, 0:HD, :] = out[:, j * width:(j + 1) * width]
        part_ref[0, j, 0, HD:, :] = slab[:, j * width:(j + 1) * width]


def on_device(queries, key_cache, value_cache, blocks, out_weight):
    shard_count = lax.axis_size("ctx")
    here_index = lax.axis_index("ctx")
    local_heads = key_cache.shape[1] // HD
    tq = queries.shape[0]
    group_size = queries.shape[1] // (local_heads * HD)
    blocks_here = key_cache.shape[0] // BLK
    query_tokens = tq * shard_count
    qblocks = query_tokens // BLK
    per_block = shard_count // qblocks
    rows = group_size * BLK
    width = rows // per_block
    extra = 16
    total_keys = shard_count * key_cache.shape[0]

    block_lists = lax.dynamic_slice_in_dim(
        blocks, lax.axis_index("kv") * local_heads, local_heads, 1
    )
    shard_first = here_index * blocks_here
    picked, inside = block_tables(block_lists, shard_first, blocks_here)
    pos0 = (shard_first * BLK - (total_keys - query_tokens)).astype(jnp.int32).reshape(1)

    qt = queries.reshape(tq, local_heads * group_size, HD).transpose(1, 0, 2)
    q_all = gather_ctx(qt)
    q_all = q_all.reshape(qblocks, per_block, local_heads, group_size, tq, HD)

    kernel = functools.partial(
        attn_kernel, heads=local_heads, rows=rows, tq=tq, score_scale=1.0 / math.sqrt(HD)
    )
    grid_spec = pltpu.PrefetchScalarGridSpec(
        num_scalar_prefetch=3,
        grid=(local_heads, qblocks),
        in_specs=[
            pl.BlockSpec((1, per_block, 1, group_size, tq, HD),
                         lambda h, b, *_: (b, 0, h, 0, 0, 0)),
            pl.BlockSpec((key_cache.shape[0], HD), lambda h, b, *_: (0, h)),
            pl.BlockSpec((value_cache.shape[0], HD), lambda h, b, *_: (0, h)),
        ],
        out_specs=pl.BlockSpec((1, per_block, 1, HD + extra, width),
                               lambda h, b, *_: (b, 0, h, 0, 0)),
        scratch_shapes=[pltpu.VMEM((MOST, BLK, rows), jnp.float32)],
    )
    part = pl.pallas_call(
        kernel,
        grid_spec=grid_spec,
        out_shape=jax.ShapeDtypeStruct(
            (qblocks, per_block, local_heads, HD + extra, width), jnp.bfloat16
        ),
        compiler_params=pltpu.CompilerParams(
            dimension_semantics=("arbitrary", "arbitrary"),
        ),
    )(picked.reshape(-1).astype(jnp.int32), inside.reshape(-1).astype(jnp.int32), pos0,
      q_all, key_cache, value_cache)

    part = part.reshape(shard_count, local_heads, HD + extra, width)
    part_in = lax.all_to_all(part, "ctx", 0, 0, tiled=True).astype(jnp.float32)
    peak_all = part_in[:, :, HD, :]
    peak_top = jnp.max(peak_all, axis=0)
    weight_all = part_in[:, :, HD + 1, :] * jnp.exp(peak_all - peak_top)
    summed = jnp.sum(weight_all[:, :, None, :] * part_in[:, :, :HD, :], axis=0)
    merged = summed / jnp.sum(weight_all, axis=0)[:, None, :]
    merged = merged.reshape(local_heads, HD, group_size, tq).transpose(3, 0, 2, 1)
    attended_heads = merged.astype(jnp.bfloat16).reshape(tq, -1)
    projected = jnp.dot(
        gather_ctx(attended_heads).reshape(-1, attended_heads.shape[1]),
        out_weight,
        preferred_element_type=jnp.float32,
    )
    return lax.psum_scatter(projected.astype(jnp.bfloat16), "kv", scatter_dimension=0, tiled=True)


def solution(mesh):
    placed = (P("ctx", "kv"), P("ctx", "kv"), P("ctx", "kv"), P(), P("kv", "ctx"))
    return jax.shard_map(
        on_device, mesh=mesh, in_specs=placed, out_specs=P("kv", "ctx"), check_vma=False
    )
```

```python
import functools
import math

import jax
import jax.numpy as jnp
from jax import lax
from jax.experimental import pallas as pl
from jax.experimental.pallas import tpu as pltpu
from jax.sharding import PartitionSpec as P

HD = 128
BLK = 128
MOST = 7

ORDERS = ((8, 4, 32, 16, 2), (32, 8, 4, 2, 16))


def gather_ctx(x):
    n = lax.axis_size("ctx")
    me = lax.axis_index("ctx")
    core = me % 2
    steps = len(ORDERS[0])
    buf = x[None]
    for step in range(steps):
        a0, a1 = ORDERS[0][step], ORDERS[1][step]
        pairs = [(c, c ^ (a0 if c % 2 == 0 else a1)) for c in range(n)]
        other = lax.ppermute(buf, "ctx", pairs)
        low = (me & jnp.where(core == 0, a0, a1)) == 0
        buf = jnp.where(low, jnp.concatenate([buf, other]), jnp.concatenate([other, buf]))
    tail = buf.shape[1:]
    outs = []
    for order in ORDERS:
        dims_bits = [order[steps - 1 - d].bit_length() - 2 for d in range(steps)]
        perm = [dims_bits.index(bb) for bb in reversed(range(steps))]
        t = buf.reshape((2,) * steps + tail)
        t = t.transpose(perm + list(range(steps, steps + len(tail))))
        outs.append(t.reshape((2 ** steps,) + tail))
    mine = jnp.where(core == 0, outs[0], outs[1])
    other = lax.ppermute(mine, "ctx", [(c, c ^ 1) for c in range(n)])
    both = jnp.where(core == 0, jnp.stack([mine, other], 1), jnp.stack([other, mine], 1))
    return both.reshape((n,) + tail)


def reduce_kv(part):
    n = lax.axis_size("kv")
    me = lax.axis_index("kv")
    bit = n // 2
    while bit >= 1:
        half = part.shape[0] // 2
        high = (me & bit) != 0
        keep = jnp.where(high, part[half:], part[:half])
        send = jnp.where(high, part[:half], part[half:])
        part = keep + lax.ppermute(send, "kv", [(i, i ^ bit) for i in range(n)])
        bit //= 2
    return part


def block_tables(block_lists, shard_first, blocks_here):
    below = jnp.sum((block_lists < shard_first).astype(jnp.int32), axis=-1)
    inside = jnp.sum(
        ((block_lists >= shard_first) & (block_lists < shard_first + blocks_here)).astype(
            jnp.int32
        ),
        axis=-1,
    )
    slot_ids = jnp.arange(MOST, dtype=jnp.int32)
    places = jnp.clip(below[..., None] + slot_ids, 0, block_lists.shape[-1] - 1)
    picked = jnp.take_along_axis(block_lists, places, axis=-1) - shard_first
    usable = slot_ids < inside[..., None]
    picked = jnp.where(usable, picked, 0)
    return picked, inside


def attn_kernel(picked_ref, count_ref, pos_ref, q_ref, k_ref, v_ref, part_ref, sc_ref,
                *, heads, rows, tq, score_scale):
    h = pl.program_id(0)
    b = pl.program_id(1)
    item = b * heads + h
    n = count_ref[item]
    q = q_ref[...].reshape(rows, HD)
    key_ids = lax.broadcasted_iota(jnp.int32, (BLK, rows), 0)
    row_ids = lax.broadcasted_iota(jnp.int32, (BLK, rows), 1)
    tok = (row_ids // (rows // (BLK // tq))) * tq + row_ids % tq
    limit = b * BLK + tok - pos_ref[0]

    def first(s, m):
        blk = picked_ref[item * MOST + s]
        start = pl.multiple_of(blk * BLK, BLK)
        kb = k_ref[pl.ds(start, BLK), :]
        sc = lax.dot_general(kb, q, (((1,), (1,)), ((), ())), preferred_element_type=jnp.float32)
        sc = sc * score_scale
        sc = jnp.where(blk * BLK + key_ids <= limit, sc, -jnp.inf)
        sc_ref[s] = sc
        return jnp.maximum(m, jnp.max(sc, axis=0, keepdims=True))

    m = lax.fori_loop(0, n, first, jnp.full((1, rows), -jnp.inf, jnp.float32))
    peak = m.astype(jnp.bfloat16).astype(jnp.float32)

    def second(s, carry):
        tot, acc = carry
        blk = picked_ref[item * MOST + s]
        start = pl.multiple_of(blk * BLK, BLK)
        vb = v_ref[pl.ds(start, BLK), :]
        w = jnp.exp(sc_ref[s] - peak)
        tot = tot + jnp.sum(w, axis=0, keepdims=True)
        acc = acc + lax.dot_general(
            vb, w.astype(jnp.bfloat16), (((0,), (0,)), ((), ())),
            preferred_element_type=jnp.float32,
        )
        return tot, acc

    tot, acc = lax.fori_loop(
        0, n, second,
        (jnp.zeros((1, rows), jnp.float32), jnp.zeros((HD, rows), jnp.float32)),
    )
    total = tot.astype(jnp.bfloat16).astype(jnp.float32)
    out = (acc / total).astype(jnp.bfloat16)
    extra = part_ref.shape[3] - HD
    slab_rows = lax.broadcasted_iota(jnp.int32, (extra, rows), 0)
    slab = jnp.where(slab_rows == 0, peak, jnp.where(slab_rows == 1, total, 0.0))
    slab = slab.astype(jnp.bfloat16)
    chunks = part_ref.shape[1]
    width = rows // chunks
    for j in range(chunks):
        part_ref[0, j, 0, 0:HD, :] = out[:, j * width:(j + 1) * width]
        part_ref[0, j, 0, HD:, :] = slab[:, j * width:(j + 1) * width]


def on_device(queries, key_cache, value_cache, blocks, out_weight):
    shard_count = lax.axis_size("ctx")
    here_index = lax.axis_index("ctx")
    local_heads = key_cache.shape[1] // HD
    tq = queries.shape[0]
    group_size = queries.shape[1] // (local_heads * HD)
    blocks_here = key_cache.shape[0] // BLK
    query_tokens = tq * shard_count
    qblocks = query_tokens // BLK
    per_block = shard_count // qblocks
    rows = group_size * BLK
    width = rows // per_block
    extra = 16
    total_keys = shard_count * key_cache.shape[0]

    block_lists = lax.dynamic_slice_in_dim(
        blocks, lax.axis_index("kv") * local_heads, local_heads, 1
    )
    shard_first = here_index * blocks_here
    picked, inside = block_tables(block_lists, shard_first, blocks_here)
    pos0 = (shard_first * BLK - (total_keys - query_tokens)).astype(jnp.int32).reshape(1)

    qt = queries.reshape(tq, local_heads * group_size, HD).transpose(1, 0, 2)
    q_all = gather_ctx(qt)
    q_all = q_all.reshape(qblocks, per_block, local_heads, group_size, tq, HD)

    kernel = functools.partial(
        attn_kernel, heads=local_heads, rows=rows, tq=tq, score_scale=1.0 / math.sqrt(HD)
    )
    grid_spec = pltpu.PrefetchScalarGridSpec(
        num_scalar_prefetch=3,
        grid=(local_heads, qblocks),
        in_specs=[
            pl.BlockSpec((1, per_block, 1, group_size, tq, HD),
                         lambda h, b, *_: (b, 0, h, 0, 0, 0)),
            pl.BlockSpec((key_cache.shape[0], HD), lambda h, b, *_: (0, h)),
            pl.BlockSpec((value_cache.shape[0], HD), lambda h, b, *_: (0, h)),
        ],
        out_specs=pl.BlockSpec((1, per_block, 1, HD + extra, width),
                               lambda h, b, *_: (b, 0, h, 0, 0)),
        scratch_shapes=[pltpu.VMEM((MOST, BLK, rows), jnp.float32)],
    )
    part = pl.pallas_call(
        kernel,
        grid_spec=grid_spec,
        out_shape=jax.ShapeDtypeStruct(
            (qblocks, per_block, local_heads, HD + extra, width), jnp.bfloat16
        ),
        compiler_params=pltpu.CompilerParams(
            dimension_semantics=("arbitrary", "arbitrary"),
        ),
    )(picked.reshape(-1).astype(jnp.int32), inside.reshape(-1).astype(jnp.int32), pos0,
      q_all, key_cache, value_cache)

    part = part.reshape(shard_count, local_heads, HD + extra, width)
    part_in = lax.all_to_all(part, "ctx", 0, 0, tiled=True).astype(jnp.float32)
    peak_all = part_in[:, :, HD, :]
    peak_top = jnp.max(peak_all, axis=0)
    weight_all = part_in[:, :, HD + 1, :] * jnp.exp(peak_all - peak_top)
    summed = jnp.sum(weight_all[:, :, None, :] * part_in[:, :, :HD, :], axis=0)
    merged = summed / jnp.sum(weight_all, axis=0)[:, None, :]
    merged = merged.reshape(local_heads, HD, group_size, tq).transpose(3, 0, 2, 1)
    attended_heads = merged.astype(jnp.bfloat16).reshape(tq, -1)
    projected = jnp.dot(
        gather_ctx(attended_heads).reshape(-1, attended_heads.shape[1]),
        out_weight,
        preferred_element_type=jnp.float32,
    )
    return reduce_kv(projected).astype(jnp.bfloat16)


def solution(mesh):
    placed = (P("ctx", "kv"), P("ctx", "kv"), P("ctx", "kv"), P(), P("kv", "ctx"))
    return jax.shard_map(
        on_device, mesh=mesh, in_specs=placed, out_specs=P("kv", "ctx"), check_vma=False
    )
```

```python
import functools
import math

import jax
import jax.numpy as jnp
from jax import lax
from jax.experimental import pallas as pl
from jax.experimental.pallas import tpu as pltpu
from jax.sharding import PartitionSpec as P

HD = 128
BLK = 128
MOST = 7

ORDERS = ((8, 4, 32, 16, 2), (32, 8, 4, 2, 16))


def gather_ctx(x):
    n = lax.axis_size("ctx")
    me = lax.axis_index("ctx")
    core = me % 2
    steps = len(ORDERS[0])
    buf = x[None]
    for step in range(steps):
        a0, a1 = ORDERS[0][step], ORDERS[1][step]
        pairs = [(c, c ^ (a0 if c % 2 == 0 else a1)) for c in range(n)]
        other = lax.ppermute(buf, "ctx", pairs)
        low = (me & jnp.where(core == 0, a0, a1)) == 0
        buf = jnp.where(low, jnp.concatenate([buf, other]), jnp.concatenate([other, buf]))
    tail = buf.shape[1:]
    outs = []
    for order in ORDERS:
        dims_bits = [order[steps - 1 - d].bit_length() - 2 for d in range(steps)]
        perm = [dims_bits.index(bb) for bb in reversed(range(steps))]
        t = buf.reshape((2,) * steps + tail)
        t = t.transpose(perm + list(range(steps, steps + len(tail))))
        outs.append(t.reshape((2 ** steps,) + tail))
    mine = jnp.where(core == 0, outs[0], outs[1])
    other = lax.ppermute(mine, "ctx", [(c, c ^ 1) for c in range(n)])
    both = jnp.where(core == 0, jnp.stack([mine, other], 1), jnp.stack([other, mine], 1))
    return both.reshape((n,) + tail)


def reduce_kv(part):
    n = lax.axis_size("kv")
    me = lax.axis_index("kv")
    bit = n // 2
    while bit >= 1:
        half = part.shape[0] // 2
        high = (me & bit) != 0
        keep = jnp.where(high, part[half:], part[:half])
        send = jnp.where(high, part[:half], part[half:])
        part = keep + lax.ppermute(send, "kv", [(i, i ^ bit) for i in range(n)])
        bit //= 2
    return part


def block_tables(block_lists, shard_first, blocks_here):
    below = jnp.sum((block_lists < shard_first).astype(jnp.int32), axis=-1)
    inside = jnp.sum(
        ((block_lists >= shard_first) & (block_lists < shard_first + blocks_here)).astype(
            jnp.int32
        ),
        axis=-1,
    )
    slot_ids = jnp.arange(MOST, dtype=jnp.int32)
    places = jnp.clip(below[..., None] + slot_ids, 0, block_lists.shape[-1] - 1)
    picked = jnp.take_along_axis(block_lists, places, axis=-1) - shard_first
    usable = slot_ids < inside[..., None]
    picked = jnp.where(usable, picked, 0)
    return picked, inside


def attn_kernel(picked_ref, count_ref, pos_ref, q_ref, k_ref, v_ref, part_ref,
                *, heads, rows, tq, score_scale, chunk):
    h = pl.program_id(0)
    b = pl.program_id(1)
    item = b * heads + h
    n = count_ref[item]
    first_query = b * BLK - pos_ref[0]
    chunks = part_ref.shape[1]
    width = rows // chunks
    extra = part_ref.shape[3] - HD
    row_groups = rows // (BLK // tq)
    for r in range(rows // chunk):
        q = q_ref[...].reshape(rows, HD)[r * chunk:(r + 1) * chunk]

        def masked(sc, blk):
            key_ids = lax.broadcasted_iota(jnp.int32, (BLK, chunk), 0)
            row_ids = lax.broadcasted_iota(jnp.int32, (BLK, chunk), 1) + r * chunk
            tok = (row_ids // row_groups) * tq + row_ids % tq
            return jnp.where(blk * BLK + key_ids <= first_query + tok, sc, -jnp.inf)

        def body(s, carry):
            m, tot, acc = carry
            blk = picked_ref[item * MOST + s]
            start = pl.multiple_of(blk * BLK, BLK)
            kb = k_ref[pl.ds(start, BLK), :]
            vb = v_ref[pl.ds(start, BLK), :]
            sc = lax.dot_general(
                kb, q, (((1,), (1,)), ((), ())), preferred_element_type=jnp.float32
            ) * score_scale
            sc = lax.cond(blk * BLK + BLK - 1 > first_query, masked, lambda x, y: x, sc, blk)
            m_new = jnp.maximum(m, jnp.max(sc, axis=0, keepdims=True))
            alpha = jnp.exp(m - m_new)
            w = jnp.exp(sc - m_new)
            tot = tot * alpha + jnp.sum(w, axis=0, keepdims=True)
            acc = acc * alpha + lax.dot_general(
                vb, w.astype(jnp.bfloat16), (((0,), (0,)), ((), ())),
                preferred_element_type=jnp.float32,
            )
            return m_new, tot, acc

        m, tot, acc = lax.fori_loop(
            0, n, body,
            (jnp.full((1, chunk), -jnp.inf, jnp.float32), jnp.zeros((1, chunk), jnp.float32),
             jnp.zeros((HD, chunk), jnp.float32)),
        )
        peak = m.astype(jnp.bfloat16).astype(jnp.float32)
        shift = jnp.exp(m - peak)
        total = (tot * shift).astype(jnp.bfloat16).astype(jnp.float32)
        out = (acc * (shift / total)).astype(jnp.bfloat16)
        slab_rows = lax.broadcasted_iota(jnp.int32, (extra, chunk), 0)
        slab = jnp.where(slab_rows == 0, peak, jnp.where(slab_rows == 1, total, 0.0))
        slab = slab.astype(jnp.bfloat16)
        for j in range(chunk // width):
            jj = r * (chunk // width) + j
            part_ref[0, jj, 0, 0:HD, :] = out[:, j * width:(j + 1) * width]
            part_ref[0, jj, 0, HD:, :] = slab[:, j * width:(j + 1) * width]


def on_device(queries, key_cache, value_cache, blocks, out_weight):
    shard_count = lax.axis_size("ctx")
    here_index = lax.axis_index("ctx")
    local_heads = key_cache.shape[1] // HD
    tq = queries.shape[0]
    group_size = queries.shape[1] // (local_heads * HD)
    blocks_here = key_cache.shape[0] // BLK
    query_tokens = tq * shard_count
    qblocks = query_tokens // BLK
    per_block = shard_count // qblocks
    rows = group_size * BLK
    width = rows // per_block
    extra = 16
    total_keys = shard_count * key_cache.shape[0]

    block_lists = lax.dynamic_slice_in_dim(
        blocks, lax.axis_index("kv") * local_heads, local_heads, 1
    )
    shard_first = here_index * blocks_here
    picked, inside = block_tables(block_lists, shard_first, blocks_here)
    pos0 = (shard_first * BLK - (total_keys - query_tokens)).astype(jnp.int32).reshape(1)

    qt = queries.reshape(tq, local_heads * group_size, HD).transpose(1, 0, 2)
    q_all = gather_ctx(qt)
    q_all = q_all.reshape(qblocks, per_block, local_heads, group_size, tq, HD)

    kernel = functools.partial(
        attn_kernel, heads=local_heads, rows=rows, tq=tq, score_scale=1.0 / math.sqrt(HD),
        chunk=2 * BLK,
    )
    grid_spec = pltpu.PrefetchScalarGridSpec(
        num_scalar_prefetch=3,
        grid=(local_heads, qblocks),
        in_specs=[
            pl.BlockSpec((1, per_block, 1, group_size, tq, HD),
                         lambda h, b, *_: (b, 0, h, 0, 0, 0)),
            pl.BlockSpec((key_cache.shape[0], HD), lambda h, b, *_: (0, h)),
            pl.BlockSpec((value_cache.shape[0], HD), lambda h, b, *_: (0, h)),
        ],
        out_specs=pl.BlockSpec((1, per_block, 1, HD + extra, width),
                               lambda h, b, *_: (b, 0, h, 0, 0)),
    )
    part = pl.pallas_call(
        kernel,
        grid_spec=grid_spec,
        out_shape=jax.ShapeDtypeStruct(
            (qblocks, per_block, local_heads, HD + extra, width), jnp.bfloat16
        ),
        compiler_params=pltpu.CompilerParams(
            dimension_semantics=("arbitrary", "arbitrary"),
        ),
    )(picked.reshape(-1).astype(jnp.int32), inside.reshape(-1).astype(jnp.int32), pos0,
      q_all, key_cache, value_cache)

    part = part.reshape(shard_count, local_heads, HD + extra, width)
    part_in = lax.all_to_all(part, "ctx", 0, 0, tiled=True).astype(jnp.float32)
    peak_all = part_in[:, :, HD, :]
    peak_top = jnp.max(peak_all, axis=0)
    weight_all = part_in[:, :, HD + 1, :] * jnp.exp(peak_all - peak_top)
    summed = jnp.sum(weight_all[:, :, None, :] * part_in[:, :, :HD, :], axis=0)
    merged = summed / jnp.sum(weight_all, axis=0)[:, None, :]
    merged = merged.reshape(local_heads, HD, group_size, tq).transpose(3, 0, 2, 1)
    attended_heads = merged.astype(jnp.bfloat16).reshape(tq, -1)
    projected = jnp.dot(
        gather_ctx(attended_heads).reshape(-1, attended_heads.shape[1]),
        out_weight,
        preferred_element_type=jnp.float32,
    )
    return reduce_kv(projected).astype(jnp.bfloat16)


def solution(mesh):
    placed = (P("ctx", "kv"), P("ctx", "kv"), P("ctx", "kv"), P(), P("kv", "ctx"))
    return jax.shard_map(
        on_device, mesh=mesh, in_specs=placed, out_specs=P("kv", "ctx"), check_vma=False
    )
```

```python
import functools
import math

import jax
import jax.numpy as jnp
from jax import lax
from jax.experimental import pallas as pl
from jax.experimental.pallas import tpu as pltpu
from jax.sharding import PartitionSpec as P

HD = 128
BLK = 128
MOST = 7

ORDERS = ((8, 4, 32, 16, 2), (32, 8, 4, 2, 16))


def gather_ctx(x):
    n = lax.axis_size("ctx")
    me = lax.axis_index("ctx")
    core = me % 2
    steps = len(ORDERS[0])
    buf = x[None]
    for step in range(steps):
        a0, a1 = ORDERS[0][step], ORDERS[1][step]
        pairs = [(c, c ^ (a0 if c % 2 == 0 else a1)) for c in range(n)]
        other = lax.ppermute(buf, "ctx", pairs)
        low = (me & jnp.where(core == 0, a0, a1)) == 0
        buf = jnp.where(low, jnp.concatenate([buf, other]), jnp.concatenate([other, buf]))
    tail = buf.shape[1:]
    outs = []
    for order in ORDERS:
        dims_bits = [order[steps - 1 - d].bit_length() - 2 for d in range(steps)]
        perm = [dims_bits.index(bb) for bb in reversed(range(steps))]
        t = buf.reshape((2,) * steps + tail)
        t = t.transpose(perm + list(range(steps, steps + len(tail))))
        outs.append(t.reshape((2 ** steps,) + tail))
    mine = jnp.where(core == 0, outs[0], outs[1])
    other = lax.ppermute(mine, "ctx", [(c, c ^ 1) for c in range(n)])
    both = jnp.where(core == 0, jnp.stack([mine, other], 1), jnp.stack([other, mine], 1))
    return both.reshape((n,) + tail)


def reduce_kv(part):
    n = lax.axis_size("kv")
    me = lax.axis_index("kv")
    bit = n // 2
    while bit >= 1:
        half = part.shape[0] // 2
        high = (me & bit) != 0
        keep = jnp.where(high, part[half:], part[:half])
        send = jnp.where(high, part[:half], part[half:])
        part = keep + lax.ppermute(send, "kv", [(i, i ^ bit) for i in range(n)])
        bit //= 2
    return part


def block_tables(block_lists, shard_first, blocks_here):
    below = jnp.sum((block_lists < shard_first).astype(jnp.int32), axis=-1)
    inside = jnp.sum(
        ((block_lists >= shard_first) & (block_lists < shard_first + blocks_here)).astype(
            jnp.int32
        ),
        axis=-1,
    )
    slot_ids = jnp.arange(MOST, dtype=jnp.int32)
    places = jnp.clip(below[..., None] + slot_ids, 0, block_lists.shape[-1] - 1)
    picked = jnp.take_along_axis(block_lists, places, axis=-1) - shard_first
    usable = slot_ids < inside[..., None]
    picked = jnp.where(usable, picked, 0)
    return picked, inside


def attn_kernel(picked_ref, count_ref, pos_ref, q_ref, k_ref, v_ref, part_ref, sc_ref,
                *, heads, rows, tq, score_scale):
    h = pl.program_id(0)
    b = pl.program_id(1)
    item = b * heads + h
    n = count_ref[item]
    q = q_ref[...].reshape(rows, HD)
    key_ids = lax.broadcasted_iota(jnp.int32, (BLK, rows), 0)
    row_ids = lax.broadcasted_iota(jnp.int32, (BLK, rows), 1)
    tok = (row_ids // (rows // (BLK // tq))) * tq + row_ids % tq
    limit = b * BLK + tok - pos_ref[0]

    def scores(s):
        blk = picked_ref[item * MOST + s]
        start = pl.multiple_of(blk * BLK, BLK)
        kb = k_ref[pl.ds(start, BLK), :]
        sc = lax.dot_general(kb, q, (((1,), (1,)), ((), ())), preferred_element_type=jnp.float32)
        return blk, sc * score_scale

    def first(s, m):
        blk, sc = scores(s)
        sc_ref[s] = sc
        return jnp.maximum(m, jnp.max(sc, axis=0, keepdims=True))

    last = jnp.maximum(n - 1, 0)
    m = lax.fori_loop(0, last, first, jnp.full((1, rows), -jnp.inf, jnp.float32))
    blk, sc = scores(last)
    sc = jnp.where(blk * BLK + key_ids <= limit, sc, -jnp.inf)
    sc_ref[last] = sc
    m = jnp.maximum(m, jnp.max(sc, axis=0, keepdims=True))
    peak = m.astype(jnp.bfloat16).astype(jnp.float32)

    def second(s, carry):
        tot, acc = carry
        blk = picked_ref[item * MOST + s]
        start = pl.multiple_of(blk * BLK, BLK)
        vb = v_ref[pl.ds(start, BLK), :]
        w = jnp.exp(sc_ref[s] - peak)
        tot = tot + jnp.sum(w, axis=0, keepdims=True)
        acc = acc + lax.dot_general(
            vb, w.astype(jnp.bfloat16), (((0,), (0,)), ((), ())),
            preferred_element_type=jnp.float32,
        )
        return tot, acc

    tot, acc = lax.fori_loop(
        0, n, second,
        (jnp.zeros((1, rows), jnp.float32), jnp.zeros((HD, rows), jnp.float32)),
    )
    total = tot.astype(jnp.bfloat16).astype(jnp.float32)
    out = (acc / total).astype(jnp.bfloat16)
    extra = part_ref.shape[3] - HD
    slab_rows = lax.broadcasted_iota(jnp.int32, (extra, rows), 0)
    slab = jnp.where(slab_rows == 0, peak, jnp.where(slab_rows == 1, total, 0.0))
    slab = slab.astype(jnp.bfloat16)
    chunks = part_ref.shape[1]
    width = rows // chunks
    for j in range(chunks):
        part_ref[0, j, 0, 0:HD, :] = out[:, j * width:(j + 1) * width]
        part_ref[0, j, 0, HD:, :] = slab[:, j * width:(j + 1) * width]


def on_device(queries, key_cache, value_cache, blocks, out_weight):
    shard_count = lax.axis_size("ctx")
    here_index = lax.axis_index("ctx")
    local_heads = key_cache.shape[1] // HD
    tq = queries.shape[0]
    group_size = queries.shape[1] // (local_heads * HD)
    blocks_here = key_cache.shape[0] // BLK
    query_tokens = tq * shard_count
    qblocks = query_tokens // BLK
    per_block = shard_count // qblocks
    rows = group_size * BLK
    width = rows // per_block
    extra = 16
    total_keys = shard_count * key_cache.shape[0]

    block_lists = lax.dynamic_slice_in_dim(
        blocks, lax.axis_index("kv") * local_heads, local_heads, 1
    )
    shard_first = here_index * blocks_here
    picked, inside = block_tables(block_lists, shard_first, blocks_here)
    pos0 = (shard_first * BLK - (total_keys - query_tokens)).astype(jnp.int32).reshape(1)

    qt = queries.reshape(tq, local_heads * group_size, HD).transpose(1, 0, 2)
    q_all = gather_ctx(qt)
    q_all = q_all.reshape(qblocks, per_block, local_heads, group_size, tq, HD)

    kernel = functools.partial(
        attn_kernel, heads=local_heads, rows=rows, tq=tq, score_scale=1.0 / math.sqrt(HD)
    )
    grid_spec = pltpu.PrefetchScalarGridSpec(
        num_scalar_prefetch=3,
        grid=(local_heads, qblocks),
        in_specs=[
            pl.BlockSpec((1, per_block, 1, group_size, tq, HD),
                         lambda h, b, *_: (b, 0, h, 0, 0, 0)),
            pl.BlockSpec((key_cache.shape[0], HD), lambda h, b, *_: (0, h)),
            pl.BlockSpec((value_cache.shape[0], HD), lambda h, b, *_: (0, h)),
        ],
        out_specs=pl.BlockSpec((1, per_block, 1, HD + extra, width),
                               lambda h, b, *_: (b, 0, h, 0, 0)),
        scratch_shapes=[pltpu.VMEM((MOST, BLK, rows), jnp.float32)],
    )
    part = pl.pallas_call(
        kernel,
        grid_spec=grid_spec,
        out_shape=jax.ShapeDtypeStruct(
            (qblocks, per_block, local_heads, HD + extra, width), jnp.bfloat16
        ),
        compiler_params=pltpu.CompilerParams(
            dimension_semantics=("arbitrary", "arbitrary"),
        ),
    )(picked.reshape(-1).astype(jnp.int32), inside.reshape(-1).astype(jnp.int32), pos0,
      q_all, key_cache, value_cache)

    part = part.reshape(shard_count, local_heads, HD + extra, width)
    part_in = lax.all_to_all(part, "ctx", 0, 0, tiled=True).astype(jnp.float32)
    peak_all = part_in[:, :, HD, :]
    peak_top = jnp.max(peak_all, axis=0)
    weight_all = part_in[:, :, HD + 1, :] * jnp.exp(peak_all - peak_top)
    summed = jnp.sum(weight_all[:, :, None, :] * part_in[:, :, :HD, :], axis=0)
    merged = summed / jnp.sum(weight_all, axis=0)[:, None, :]
    merged = merged.reshape(local_heads, HD, group_size, tq).transpose(3, 0, 2, 1)
    attended_heads = merged.astype(jnp.bfloat16).reshape(tq, -1)
    projected = jnp.dot(
        gather_ctx(attended_heads).reshape(-1, attended_heads.shape[1]),
        out_weight,
        preferred_element_type=jnp.float32,
    )
    return reduce_kv(projected).astype(jnp.bfloat16)


def solution(mesh):
    placed = (P("ctx", "kv"), P("ctx", "kv"), P("ctx", "kv"), P(), P("kv", "ctx"))
    return jax.shard_map(
        on_device, mesh=mesh, in_specs=placed, out_specs=P("kv", "ctx"), check_vma=False
    )
```

```python
import functools
import math

import jax
import jax.numpy as jnp
from jax import lax
from jax.experimental import pallas as pl
from jax.experimental.pallas import tpu as pltpu
from jax.sharding import PartitionSpec as P

HD = 128
BLK = 128
MOST = 7

ORDERS = ((8, 4, 32, 16, 2), (32, 8, 4, 2, 16))


def gather_ctx(x):
    n = lax.axis_size("ctx")
    me = lax.axis_index("ctx")
    core = me % 2
    steps = len(ORDERS[0])
    buf = x[None]
    for step in range(steps):
        a0, a1 = ORDERS[0][step], ORDERS[1][step]
        pairs = [(c, c ^ (a0 if c % 2 == 0 else a1)) for c in range(n)]
        other = lax.ppermute(buf, "ctx", pairs)
        low = (me & jnp.where(core == 0, a0, a1)) == 0
        buf = jnp.where(low, jnp.concatenate([buf, other]), jnp.concatenate([other, buf]))
    tail = buf.shape[1:]
    outs = []
    for order in ORDERS:
        dims_bits = [order[steps - 1 - d].bit_length() - 2 for d in range(steps)]
        perm = [dims_bits.index(bb) for bb in reversed(range(steps))]
        t = buf.reshape((2,) * steps + tail)
        t = t.transpose(perm + list(range(steps, steps + len(tail))))
        outs.append(t.reshape((2 ** steps,) + tail))
    mine = jnp.where(core == 0, outs[0], outs[1])
    other = lax.ppermute(mine, "ctx", [(c, c ^ 1) for c in range(n)])
    both = jnp.where(core == 0, jnp.stack([mine, other], 1), jnp.stack([other, mine], 1))
    return both.reshape((n,) + tail)


def reduce_kv(part):
    n = lax.axis_size("kv")
    me = lax.axis_index("kv")
    bit = n // 2
    while bit >= 1:
        half = part.shape[0] // 2
        high = (me & bit) != 0
        keep = jnp.where(high, part[half:], part[:half])
        send = jnp.where(high, part[:half], part[half:])
        part = keep + lax.ppermute(send, "kv", [(i, i ^ bit) for i in range(n)])
        bit //= 2
    return part


def block_tables(block_lists, shard_first, blocks_here):
    below = jnp.sum((block_lists < shard_first).astype(jnp.int32), axis=-1)
    inside = jnp.sum(
        ((block_lists >= shard_first) & (block_lists < shard_first + blocks_here)).astype(
            jnp.int32
        ),
        axis=-1,
    )
    slot_ids = jnp.arange(MOST, dtype=jnp.int32)
    places = jnp.clip(below[..., None] + slot_ids, 0, block_lists.shape[-1] - 1)
    picked = jnp.take_along_axis(block_lists, places, axis=-1) - shard_first
    usable = slot_ids < inside[..., None]
    picked = jnp.where(usable, picked, 0)
    return picked, inside


def attn_kernel(picked_ref, count_ref, pos_ref, q_ref, k_ref, v_ref, part_ref, sc_ref,
                *, heads, rows, tq, score_scale):
    h = pl.program_id(0)
    b = pl.program_id(1)
    item = b * heads + h
    n = count_ref[item]
    q_t = q_ref[...].reshape(rows, HD).astype(jnp.float32).T.astype(jnp.bfloat16)
    key_ids = lax.broadcasted_iota(jnp.int32, (BLK, rows), 0)
    row_ids = lax.broadcasted_iota(jnp.int32, (BLK, rows), 1)
    tok = (row_ids // (rows // (BLK // tq))) * tq + row_ids % tq
    limit = b * BLK + tok - pos_ref[0]

    def scores(s):
        blk = picked_ref[item * MOST + s]
        start = pl.multiple_of(blk * BLK, BLK)
        kb = k_ref[pl.ds(start, BLK), :]
        sc = jnp.dot(kb, q_t, preferred_element_type=jnp.float32)
        return blk, sc * score_scale

    def first(s, m):
        blk, sc = scores(s)
        sc_ref[s] = sc
        return jnp.maximum(m, jnp.max(sc, axis=0, keepdims=True))

    last = jnp.maximum(n - 1, 0)
    m = lax.fori_loop(0, last, first, jnp.full((1, rows), -jnp.inf, jnp.float32))
    blk, sc = scores(last)
    sc = jnp.where(blk * BLK + key_ids <= limit, sc, -jnp.inf)
    sc_ref[last] = sc
    m = jnp.maximum(m, jnp.max(sc, axis=0, keepdims=True))
    peak = m.astype(jnp.bfloat16).astype(jnp.float32)

    def second(s, carry):
        tot, acc = carry
        blk = picked_ref[item * MOST + s]
        start = pl.multiple_of(blk * BLK, BLK)
        vb = v_ref[pl.ds(start, BLK), :]
        w = jnp.exp(sc_ref[s] - peak)
        tot = tot + jnp.sum(w, axis=0, keepdims=True)
        acc = acc + lax.dot_general(
            vb, w.astype(jnp.bfloat16), (((0,), (0,)), ((), ())),
            preferred_element_type=jnp.float32,
        )
        return tot, acc

    tot, acc = lax.fori_loop(
        0, n, second,
        (jnp.zeros((1, rows), jnp.float32), jnp.zeros((HD, rows), jnp.float32)),
    )
    total = tot.astype(jnp.bfloat16).astype(jnp.float32)
    out = (acc / total).astype(jnp.bfloat16)
    extra = part_ref.shape[3] - HD
    slab_rows = lax.broadcasted_iota(jnp.int32, (extra, rows), 0)
    slab = jnp.where(slab_rows == 0, peak, jnp.where(slab_rows == 1, total, 0.0))
    slab = slab.astype(jnp.bfloat16)
    chunks = part_ref.shape[1]
    width = rows // chunks
    for j in range(chunks):
        part_ref[0, j, 0, 0:HD, :] = out[:, j * width:(j + 1) * width]
        part_ref[0, j, 0, HD:, :] = slab[:, j * width:(j + 1) * width]


def on_device(queries, key_cache, value_cache, blocks, out_weight):
    shard_count = lax.axis_size("ctx")
    here_index = lax.axis_index("ctx")
    local_heads = key_cache.shape[1] // HD
    tq = queries.shape[0]
    group_size = queries.shape[1] // (local_heads * HD)
    blocks_here = key_cache.shape[0] // BLK
    query_tokens = tq * shard_count
    qblocks = query_tokens // BLK
    per_block = shard_count // qblocks
    rows = group_size * BLK
    width = rows // per_block
    extra = 16
    total_keys = shard_count * key_cache.shape[0]

    block_lists = lax.dynamic_slice_in_dim(
        blocks, lax.axis_index("kv") * local_heads, local_heads, 1
    )
    shard_first = here_index * blocks_here
    picked, inside = block_tables(block_lists, shard_first, blocks_here)
    pos0 = (shard_first * BLK - (total_keys - query_tokens)).astype(jnp.int32).reshape(1)

    qt = queries.reshape(tq, local_heads * group_size, HD).transpose(1, 0, 2)
    q_all = gather_ctx(qt)
    q_all = q_all.reshape(qblocks, per_block, local_heads, group_size, tq, HD)

    kernel = functools.partial(
        attn_kernel, heads=local_heads, rows=rows, tq=tq, score_scale=1.0 / math.sqrt(HD)
    )
    grid_spec = pltpu.PrefetchScalarGridSpec(
        num_scalar_prefetch=3,
        grid=(local_heads, qblocks),
        in_specs=[
            pl.BlockSpec((1, per_block, 1, group_size, tq, HD),
                         lambda h, b, *_: (b, 0, h, 0, 0, 0)),
            pl.BlockSpec((key_cache.shape[0], HD), lambda h, b, *_: (0, h)),
            pl.BlockSpec((value_cache.shape[0], HD), lambda h, b, *_: (0, h)),
        ],
        out_specs=pl.BlockSpec((1, per_block, 1, HD + extra, width),
                               lambda h, b, *_: (b, 0, h, 0, 0)),
        scratch_shapes=[pltpu.VMEM((MOST, BLK, rows), jnp.float32)],
    )
    part = pl.pallas_call(
        kernel,
        grid_spec=grid_spec,
        out_shape=jax.ShapeDtypeStruct(
            (qblocks, per_block, local_heads, HD + extra, width), jnp.bfloat16
        ),
        compiler_params=pltpu.CompilerParams(
            dimension_semantics=("arbitrary", "arbitrary"),
        ),
    )(picked.reshape(-1).astype(jnp.int32), inside.reshape(-1).astype(jnp.int32), pos0,
      q_all, key_cache, value_cache)

    part = part.reshape(shard_count, local_heads, HD + extra, width)
    part_in = lax.all_to_all(part, "ctx", 0, 0, tiled=True).astype(jnp.float32)
    peak_all = part_in[:, :, HD, :]
    peak_top = jnp.max(peak_all, axis=0)
    weight_all = part_in[:, :, HD + 1, :] * jnp.exp(peak_all - peak_top)
    summed = jnp.sum(weight_all[:, :, None, :] * part_in[:, :, :HD, :], axis=0)
    merged = summed / jnp.sum(weight_all, axis=0)[:, None, :]
    merged = merged.reshape(local_heads, HD, group_size, tq).transpose(3, 0, 2, 1)
    attended_heads = merged.astype(jnp.bfloat16).reshape(tq, -1)
    projected = jnp.dot(
        gather_ctx(attended_heads).reshape(-1, attended_heads.shape[1]),
        out_weight,
        preferred_element_type=jnp.float32,
    )
    return reduce_kv(projected).astype(jnp.bfloat16)


def solution(mesh):
    placed = (P("ctx", "kv"), P("ctx", "kv"), P("ctx", "kv"), P(), P("kv", "ctx"))
    return jax.shard_map(
        on_device, mesh=mesh, in_specs=placed, out_specs=P("kv", "ctx"), check_vma=False
    )
```

```python
import functools
import math

import jax
import jax.numpy as jnp
from jax import lax
from jax.experimental import pallas as pl
from jax.experimental.pallas import tpu as pltpu
from jax.sharding import PartitionSpec as P

HD = 128
BLK = 128
MOST = 7

ORDERS = ((8, 4, 32, 16, 2), (32, 8, 4, 2, 16))


def gather_ctx(x):
    n = lax.axis_size("ctx")
    me = lax.axis_index("ctx")
    core = me % 2
    steps = len(ORDERS[0])
    buf = x[None]
    for step in range(steps):
        a0, a1 = ORDERS[0][step], ORDERS[1][step]
        pairs = [(c, c ^ (a0 if c % 2 == 0 else a1)) for c in range(n)]
        other = lax.ppermute(buf, "ctx", pairs)
        low = (me & jnp.where(core == 0, a0, a1)) == 0
        buf = jnp.where(low, jnp.concatenate([buf, other]), jnp.concatenate([other, buf]))
    tail = buf.shape[1:]
    outs = []
    for order in ORDERS:
        dims_bits = [order[steps - 1 - d].bit_length() - 2 for d in range(steps)]
        perm = [dims_bits.index(bb) for bb in reversed(range(steps))]
        t = buf.reshape((2,) * steps + tail)
        t = t.transpose(perm + list(range(steps, steps + len(tail))))
        outs.append(t.reshape((2 ** steps,) + tail))
    mine = jnp.where(core == 0, outs[0], outs[1])
    other = lax.ppermute(mine, "ctx", [(c, c ^ 1) for c in range(n)])
    both = jnp.where(core == 0, jnp.stack([mine, other], 1), jnp.stack([other, mine], 1))
    return both.reshape((n,) + tail)


def reduce_kv(part):
    n = lax.axis_size("kv")
    me = lax.axis_index("kv")
    bit = n // 2
    while bit >= 1:
        half = part.shape[0] // 2
        high = (me & bit) != 0
        keep = jnp.where(high, part[half:], part[:half])
        send = jnp.where(high, part[:half], part[half:])
        part = keep + lax.ppermute(send, "kv", [(i, i ^ bit) for i in range(n)])
        bit //= 2
    return part


def block_tables(block_lists, shard_first, blocks_here):
    below = jnp.sum((block_lists < shard_first).astype(jnp.int32), axis=-1)
    inside = jnp.sum(
        ((block_lists >= shard_first) & (block_lists < shard_first + blocks_here)).astype(
            jnp.int32
        ),
        axis=-1,
    )
    slot_ids = jnp.arange(MOST, dtype=jnp.int32)
    places = jnp.clip(below[..., None] + slot_ids, 0, block_lists.shape[-1] - 1)
    picked = jnp.take_along_axis(block_lists, places, axis=-1) - shard_first
    usable = slot_ids < inside[..., None]
    picked = jnp.where(usable, picked, 0)
    return picked, inside


def attn_kernel(picked_ref, count_ref, pos_ref, q_ref, k_ref, v_ref, part_ref, sc_ref,
                vsel_ref, w_ref, *, heads, rows, tq, score_scale):
    h = pl.program_id(0)
    b = pl.program_id(1)
    item = b * heads + h
    n = count_ref[item]
    q_t = q_ref[...].reshape(rows, HD).astype(jnp.float32).T.astype(jnp.bfloat16)
    key_ids = lax.broadcasted_iota(jnp.int32, (BLK, rows), 0)
    row_ids = lax.broadcasted_iota(jnp.int32, (BLK, rows), 1)
    tok = (row_ids // (rows // (BLK // tq))) * tq + row_ids % tq
    limit = b * BLK + tok - pos_ref[0]

    def scores(s):
        blk = picked_ref[item * MOST + s]
        start = pl.multiple_of(blk * BLK, BLK)
        kb = k_ref[pl.ds(start, BLK), :]
        sc = jnp.dot(kb, q_t, preferred_element_type=jnp.float32)
        return blk, sc * score_scale

    def first(s, m):
        blk, sc = scores(s)
        sc_ref[s] = sc
        return jnp.maximum(m, jnp.max(sc, axis=0, keepdims=True))

    last = jnp.maximum(n - 1, 0)
    m = lax.fori_loop(0, last, first, jnp.full((1, rows), -jnp.inf, jnp.float32))
    blk, sc = scores(last)
    sc = jnp.where(blk * BLK + key_ids <= limit, sc, -jnp.inf)
    sc_ref[last] = sc
    m = jnp.maximum(m, jnp.max(sc, axis=0, keepdims=True))
    peak = m.astype(jnp.bfloat16).astype(jnp.float32)

    def second(s, tot):
        blk = picked_ref[item * MOST + s]
        start = pl.multiple_of(blk * BLK, BLK)
        vsel_ref[s] = v_ref[pl.ds(start, BLK), :]
        w = jnp.exp(sc_ref[s] - peak)
        w_ref[s] = w.astype(jnp.bfloat16)
        return tot + jnp.sum(w, axis=0, keepdims=True)

    tot = lax.fori_loop(0, n, second, jnp.zeros((1, rows), jnp.float32))

    def blank(s, carry):
        vsel_ref[s] = jnp.zeros((BLK, HD), jnp.bfloat16)
        w_ref[s] = jnp.zeros((BLK, rows), jnp.bfloat16)
        return carry

    lax.fori_loop(n, MOST, blank, 0)
    acc = lax.dot_general(
        vsel_ref[...].reshape(MOST * BLK, HD), w_ref[...].reshape(MOST * BLK, rows),
        (((0,), (0,)), ((), ())), preferred_element_type=jnp.float32,
    )
    total = tot.astype(jnp.bfloat16).astype(jnp.float32)
    out = (acc / total).astype(jnp.bfloat16)
    extra = part_ref.shape[3] - HD
    slab_rows = lax.broadcasted_iota(jnp.int32, (extra, rows), 0)
    slab = jnp.where(slab_rows == 0, peak, jnp.where(slab_rows == 1, total, 0.0))
    slab = slab.astype(jnp.bfloat16)
    chunks = part_ref.shape[1]
    width = rows // chunks
    for j in range(chunks):
        part_ref[0, j, 0, 0:HD, :] = out[:, j * width:(j + 1) * width]
        part_ref[0, j, 0, HD:, :] = slab[:, j * width:(j + 1) * width]


def on_device(queries, key_cache, value_cache, blocks, out_weight):
    shard_count = lax.axis_size("ctx")
    here_index = lax.axis_index("ctx")
    local_heads = key_cache.shape[1] // HD
    tq = queries.shape[0]
    group_size = queries.shape[1] // (local_heads * HD)
    blocks_here = key_cache.shape[0] // BLK
    query_tokens = tq * shard_count
    qblocks = query_tokens // BLK
    per_block = shard_count // qblocks
    rows = group_size * BLK
    width = rows // per_block
    extra = 16
    total_keys = shard_count * key_cache.shape[0]

    block_lists = lax.dynamic_slice_in_dim(
        blocks, lax.axis_index("kv") * local_heads, local_heads, 1
    )
    shard_first = here_index * blocks_here
    picked, inside = block_tables(block_lists, shard_first, blocks_here)
    pos0 = (shard_first * BLK - (total_keys - query_tokens)).astype(jnp.int32).reshape(1)

    qt = queries.reshape(tq, local_heads * group_size, HD).transpose(1, 0, 2)
    q_all = gather_ctx(qt)
    q_all = q_all.reshape(qblocks, per_block, local_heads, group_size, tq, HD)

    kernel = functools.partial(
        attn_kernel, heads=local_heads, rows=rows, tq=tq, score_scale=1.0 / math.sqrt(HD)
    )
    grid_spec = pltpu.PrefetchScalarGridSpec(
        num_scalar_prefetch=3,
        grid=(local_heads, qblocks),
        in_specs=[
            pl.BlockSpec((1, per_block, 1, group_size, tq, HD),
                         lambda h, b, *_: (b, 0, h, 0, 0, 0)),
            pl.BlockSpec((key_cache.shape[0], HD), lambda h, b, *_: (0, h)),
            pl.BlockSpec((value_cache.shape[0], HD), lambda h, b, *_: (0, h)),
        ],
        out_specs=pl.BlockSpec((1, per_block, 1, HD + extra, width),
                               lambda h, b, *_: (b, 0, h, 0, 0)),
        scratch_shapes=[
            pltpu.VMEM((MOST, BLK, rows), jnp.float32),
            pltpu.VMEM((MOST, BLK, HD), jnp.bfloat16),
            pltpu.VMEM((MOST, BLK, rows), jnp.bfloat16),
        ],
    )
    part = pl.pallas_call(
        kernel,
        grid_spec=grid_spec,
        out_shape=jax.ShapeDtypeStruct(
            (qblocks, per_block, local_heads, HD + extra, width), jnp.bfloat16
        ),
        compiler_params=pltpu.CompilerParams(
            dimension_semantics=("arbitrary", "arbitrary"),
        ),
    )(picked.reshape(-1).astype(jnp.int32), inside.reshape(-1).astype(jnp.int32), pos0,
      q_all, key_cache, value_cache)

    part = part.reshape(shard_count, local_heads, HD + extra, width)
    part_in = lax.all_to_all(part, "ctx", 0, 0, tiled=True).astype(jnp.float32)
    peak_all = part_in[:, :, HD, :]
    peak_top = jnp.max(peak_all, axis=0)
    weight_all = part_in[:, :, HD + 1, :] * jnp.exp(peak_all - peak_top)
    summed = jnp.sum(weight_all[:, :, None, :] * part_in[:, :, :HD, :], axis=0)
    merged = summed / jnp.sum(weight_all, axis=0)[:, None, :]
    merged = merged.reshape(local_heads, HD, group_size, tq).transpose(3, 0, 2, 1)
    attended_heads = merged.astype(jnp.bfloat16).reshape(tq, -1)
    projected = jnp.dot(
        gather_ctx(attended_heads).reshape(-1, attended_heads.shape[1]),
        out_weight,
        preferred_element_type=jnp.float32,
    )
    return reduce_kv(projected).astype(jnp.bfloat16)


def solution(mesh):
    placed = (P("ctx", "kv"), P("ctx", "kv"), P("ctx", "kv"), P(), P("kv", "ctx"))
    return jax.shard_map(
        on_device, mesh=mesh, in_specs=placed, out_specs=P("kv", "ctx"), check_vma=False
    )
```

```python
import functools
import math

import jax
import jax.numpy as jnp
from jax import lax
from jax.experimental import pallas as pl
from jax.experimental.pallas import tpu as pltpu
from jax.sharding import PartitionSpec as P

HD = 128
BLK = 128
MOST = 7

ORDERS = ((8, 4, 32, 16, 2), (32, 8, 4, 2, 16))


def gather_ctx(x):
    n = lax.axis_size("ctx")
    me = lax.axis_index("ctx")
    core = me % 2
    steps = len(ORDERS[0])
    buf = x[None]
    for step in range(steps):
        a0, a1 = ORDERS[0][step], ORDERS[1][step]
        pairs = [(c, c ^ (a0 if c % 2 == 0 else a1)) for c in range(n)]
        other = lax.ppermute(buf, "ctx", pairs)
        low = (me & jnp.where(core == 0, a0, a1)) == 0
        buf = jnp.where(low, jnp.concatenate([buf, other]), jnp.concatenate([other, buf]))
    tail = buf.shape[1:]
    outs = []
    for order in ORDERS:
        dims_bits = [order[steps - 1 - d].bit_length() - 2 for d in range(steps)]
        perm = [dims_bits.index(bb) for bb in reversed(range(steps))]
        t = buf.reshape((2,) * steps + tail)
        t = t.transpose(perm + list(range(steps, steps + len(tail))))
        outs.append(t.reshape((2 ** steps,) + tail))
    mine = jnp.where(core == 0, outs[0], outs[1])
    other = lax.ppermute(mine, "ctx", [(c, c ^ 1) for c in range(n)])
    both = jnp.where(core == 0, jnp.stack([mine, other], 1), jnp.stack([other, mine], 1))
    return both.reshape((n,) + tail)


def reduce_kv(part):
    n = lax.axis_size("kv")
    me = lax.axis_index("kv")
    bit = n // 2
    while bit >= 1:
        half = part.shape[0] // 2
        high = (me & bit) != 0
        keep = jnp.where(high, part[half:], part[:half])
        send = jnp.where(high, part[:half], part[half:])
        part = keep + lax.ppermute(send, "kv", [(i, i ^ bit) for i in range(n)])
        bit //= 2
    return part


def block_tables(block_lists, shard_first, blocks_here):
    below = jnp.sum((block_lists < shard_first).astype(jnp.int32), axis=-1)
    inside = jnp.sum(
        ((block_lists >= shard_first) & (block_lists < shard_first + blocks_here)).astype(
            jnp.int32
        ),
        axis=-1,
    )
    slot_ids = jnp.arange(MOST, dtype=jnp.int32)
    places = jnp.clip(below[..., None] + slot_ids, 0, block_lists.shape[-1] - 1)
    picked = jnp.take_along_axis(block_lists, places, axis=-1) - shard_first
    usable = slot_ids < inside[..., None]
    picked = jnp.where(usable, picked, 0)
    return picked, inside


def attn_kernel(picked_ref, count_ref, pos_ref, q_ref, k_ref, v_ref, part_ref, sc_ref,
                vsel_ref, w_ref, *, heads, rows, tq, score_scale):
    h = pl.program_id(0)
    b = pl.program_id(1)
    item = b * heads + h
    n = count_ref[item]
    q_t = q_ref[...].reshape(rows, HD).astype(jnp.float32).T.astype(jnp.bfloat16)
    key_ids = lax.broadcasted_iota(jnp.int32, (BLK, rows), 0)
    row_ids = lax.broadcasted_iota(jnp.int32, (BLK, rows), 1)
    tok = (row_ids // (rows // (BLK // tq))) * tq + row_ids % tq
    limit = b * BLK + tok - pos_ref[0]

    def scores(s):
        blk = picked_ref[item * MOST + s]
        start = pl.multiple_of(blk * BLK, BLK)
        kb = k_ref[pl.ds(start, BLK), :]
        return blk, jnp.dot(kb, q_t, preferred_element_type=jnp.float32)

    def first(s, m):
        blk, sc = scores(s)
        sc_ref[s] = sc
        return jnp.maximum(m, jnp.max(sc, axis=0, keepdims=True))

    last = jnp.maximum(n - 1, 0)
    m = lax.fori_loop(0, last, first, jnp.full((1, rows), -jnp.inf, jnp.float32))
    blk, sc = scores(last)
    sc = jnp.where(blk * BLK + key_ids <= limit, sc, -jnp.inf)
    sc_ref[last] = sc
    m = jnp.maximum(m, jnp.max(sc, axis=0, keepdims=True))
    peak = (m * score_scale).astype(jnp.bfloat16).astype(jnp.float32)
    offset = peak / score_scale
    factor = score_scale * math.log2(math.e)
    ones = jnp.ones((BLK, HD), jnp.bfloat16)

    def second(s, carry):
        blk = picked_ref[item * MOST + s]
        start = pl.multiple_of(blk * BLK, BLK)
        vsel_ref[s] = jnp.concatenate([v_ref[pl.ds(start, BLK), :], ones], axis=1)
        w_ref[s] = jnp.exp2((sc_ref[s] - offset) * factor).astype(jnp.bfloat16)
        return carry

    lax.fori_loop(0, n, second, 0)

    def blank(s, carry):
        vsel_ref[s] = jnp.zeros((BLK, 2 * HD), jnp.bfloat16)
        w_ref[s] = jnp.zeros((BLK, rows), jnp.bfloat16)
        return carry

    lax.fori_loop(n, MOST, blank, 0)
    acc = lax.dot_general(
        vsel_ref[...].reshape(MOST * BLK, 2 * HD), w_ref[...].reshape(MOST * BLK, rows),
        (((0,), (0,)), ((), ())), preferred_element_type=jnp.float32,
    )
    tot = acc[HD:HD + 1]
    acc = acc[:HD]
    total = tot.astype(jnp.bfloat16).astype(jnp.float32)
    out = (acc / total).astype(jnp.bfloat16)
    extra = part_ref.shape[3] - HD
    slab_rows = lax.broadcasted_iota(jnp.int32, (extra, rows), 0)
    slab = jnp.where(slab_rows == 0, peak, jnp.where(slab_rows == 1, total, 0.0))
    slab = slab.astype(jnp.bfloat16)
    chunks = part_ref.shape[1]
    width = rows // chunks
    for j in range(chunks):
        part_ref[0, j, 0, 0:HD, :] = out[:, j * width:(j + 1) * width]
        part_ref[0, j, 0, HD:, :] = slab[:, j * width:(j + 1) * width]


def on_device(queries, key_cache, value_cache, blocks, out_weight):
    shard_count = lax.axis_size("ctx")
    here_index = lax.axis_index("ctx")
    local_heads = key_cache.shape[1] // HD
    tq = queries.shape[0]
    group_size = queries.shape[1] // (local_heads * HD)
    blocks_here = key_cache.shape[0] // BLK
    query_tokens = tq * shard_count
    qblocks = query_tokens // BLK
    per_block = shard_count // qblocks
    rows = group_size * BLK
    width = rows // per_block
    extra = 16
    total_keys = shard_count * key_cache.shape[0]

    block_lists = lax.dynamic_slice_in_dim(
        blocks, lax.axis_index("kv") * local_heads, local_heads, 1
    )
    shard_first = here_index * blocks_here
    picked, inside = block_tables(block_lists, shard_first, blocks_here)
    pos0 = (shard_first * BLK - (total_keys - query_tokens)).astype(jnp.int32).reshape(1)

    qt = queries.reshape(tq, local_heads * group_size, HD).transpose(1, 0, 2)
    q_all = gather_ctx(qt)
    q_all = q_all.reshape(qblocks, per_block, local_heads, group_size, tq, HD)

    kernel = functools.partial(
        attn_kernel, heads=local_heads, rows=rows, tq=tq, score_scale=1.0 / math.sqrt(HD)
    )
    grid_spec = pltpu.PrefetchScalarGridSpec(
        num_scalar_prefetch=3,
        grid=(local_heads, qblocks),
        in_specs=[
            pl.BlockSpec((1, per_block, 1, group_size, tq, HD),
                         lambda h, b, *_: (b, 0, h, 0, 0, 0)),
            pl.BlockSpec((key_cache.shape[0], HD), lambda h, b, *_: (0, h)),
            pl.BlockSpec((value_cache.shape[0], HD), lambda h, b, *_: (0, h)),
        ],
        out_specs=pl.BlockSpec((1, per_block, 1, HD + extra, width),
                               lambda h, b, *_: (b, 0, h, 0, 0)),
        scratch_shapes=[
            pltpu.VMEM((MOST, BLK, rows), jnp.float32),
            pltpu.VMEM((MOST, BLK, 2 * HD), jnp.bfloat16),
            pltpu.VMEM((MOST, BLK, rows), jnp.bfloat16),
        ],
    )
    part = pl.pallas_call(
        kernel,
        grid_spec=grid_spec,
        out_shape=jax.ShapeDtypeStruct(
            (qblocks, per_block, local_heads, HD + extra, width), jnp.bfloat16
        ),
        compiler_params=pltpu.CompilerParams(
            dimension_semantics=("arbitrary", "arbitrary"),
        ),
    )(picked.reshape(-1).astype(jnp.int32), inside.reshape(-1).astype(jnp.int32), pos0,
      q_all, key_cache, value_cache)

    part = part.reshape(shard_count, local_heads, HD + extra, width)
    part_in = lax.all_to_all(part, "ctx", 0, 0, tiled=True).astype(jnp.float32)
    peak_all = part_in[:, :, HD, :]
    peak_top = jnp.max(peak_all, axis=0)
    weight_all = part_in[:, :, HD + 1, :] * jnp.exp(peak_all - peak_top)
    summed = jnp.sum(weight_all[:, :, None, :] * part_in[:, :, :HD, :], axis=0)
    merged = summed / jnp.sum(weight_all, axis=0)[:, None, :]
    merged = merged.reshape(local_heads, HD, group_size, tq).transpose(3, 0, 2, 1)
    attended_heads = merged.astype(jnp.bfloat16).reshape(tq, -1)
    projected = jnp.dot(
        gather_ctx(attended_heads).reshape(-1, attended_heads.shape[1]),
        out_weight,
        preferred_element_type=jnp.float32,
    )
    return reduce_kv(projected).astype(jnp.bfloat16)


def solution(mesh):
    placed = (P("ctx", "kv"), P("ctx", "kv"), P("ctx", "kv"), P(), P("kv", "ctx"))
    return jax.shard_map(
        on_device, mesh=mesh, in_specs=placed, out_specs=P("kv", "ctx"), check_vma=False
    )
```

```python
import functools
import math

import jax
import jax.numpy as jnp
from jax import lax
from jax.experimental import pallas as pl
from jax.experimental.pallas import tpu as pltpu
from jax.sharding import PartitionSpec as P

HD = 128
BLK = 128
MOST = 7

ORDERS = ((8, 4, 32, 16, 2), (32, 8, 4, 2, 16))


def gather_ctx(x, tie=None):
    n = lax.axis_size("ctx")
    me = lax.axis_index("ctx")
    core = me % 2
    steps = len(ORDERS[0])
    buf = x[None]
    for step in range(steps):
        a0, a1 = ORDERS[0][step], ORDERS[1][step]
        pairs = [(c, c ^ (a0 if c % 2 == 0 else a1)) for c in range(n)]
        other = lax.ppermute(buf, "ctx", pairs)
        low = (me & jnp.where(core == 0, a0, a1)) == 0
        buf = jnp.where(low, jnp.concatenate([buf, other]), jnp.concatenate([other, buf]))
        if step == 0 and tie is not None:
            buf, tie = lax.optimization_barrier((buf, tie))
    tail = buf.shape[1:]
    outs = []
    for order in ORDERS:
        dims_bits = [order[steps - 1 - d].bit_length() - 2 for d in range(steps)]
        perm = [dims_bits.index(bb) for bb in reversed(range(steps))]
        t = buf.reshape((2,) * steps + tail)
        t = t.transpose(perm + list(range(steps, steps + len(tail))))
        outs.append(t.reshape((2 ** steps,) + tail))
    mine = jnp.where(core == 0, outs[0], outs[1])
    other = lax.ppermute(mine, "ctx", [(c, c ^ 1) for c in range(n)])
    both = jnp.where(core == 0, jnp.stack([mine, other], 1), jnp.stack([other, mine], 1))
    if tie is None:
        return both.reshape((n,) + tail)
    return both.reshape((n,) + tail), tie


def reduce_kv(part):
    n = lax.axis_size("kv")
    me = lax.axis_index("kv")
    bit = n // 2
    while bit >= 1:
        half = part.shape[0] // 2
        high = (me & bit) != 0
        keep = jnp.where(high, part[half:], part[:half])
        send = jnp.where(high, part[:half], part[half:])
        part = keep + lax.ppermute(send, "kv", [(i, i ^ bit) for i in range(n)])
        bit //= 2
    return part


def block_tables(block_lists, shard_first, blocks_here):
    below = jnp.sum((block_lists < shard_first).astype(jnp.int32), axis=-1)
    inside = jnp.sum(
        ((block_lists >= shard_first) & (block_lists < shard_first + blocks_here)).astype(
            jnp.int32
        ),
        axis=-1,
    )
    slot_ids = jnp.arange(MOST, dtype=jnp.int32)
    places = jnp.clip(below[..., None] + slot_ids, 0, block_lists.shape[-1] - 1)
    picked = jnp.take_along_axis(block_lists, places, axis=-1) - shard_first
    usable = slot_ids < inside[..., None]
    picked = jnp.where(usable, picked, 0)
    return picked, inside


def attn_kernel(picked_ref, count_ref, pos_ref, q_ref, k_ref, v_ref, part_ref, sc_ref,
                vsel_ref, w_ref, *, heads, rows, tq, score_scale):
    h = pl.program_id(0)
    b = pl.program_id(1)
    item = b * heads + h
    n = count_ref[item]
    q_t = q_ref[...].reshape(rows, HD).astype(jnp.float32).T.astype(jnp.bfloat16)
    key_ids = lax.broadcasted_iota(jnp.int32, (BLK, rows), 0)
    row_ids = lax.broadcasted_iota(jnp.int32, (BLK, rows), 1)
    tok = (row_ids // (rows // (BLK // tq))) * tq + row_ids % tq
    limit = b * BLK + tok - pos_ref[0]

    def scores(s):
        blk = picked_ref[item * MOST + s]
        start = pl.multiple_of(blk * BLK, BLK)
        kb = k_ref[pl.ds(start, BLK), :]
        sc = jnp.dot(kb, q_t, preferred_element_type=jnp.float32)
        return blk, sc * score_scale

    def first(s, m):
        blk, sc = scores(s)
        sc_ref[s] = sc
        return jnp.maximum(m, jnp.max(sc, axis=0, keepdims=True))

    last = jnp.maximum(n - 1, 0)
    m = lax.fori_loop(0, last, first, jnp.full((1, rows), -jnp.inf, jnp.float32))
    blk, sc = scores(last)
    sc = jnp.where(blk * BLK + key_ids <= limit, sc, -jnp.inf)
    sc_ref[last] = sc
    m = jnp.maximum(m, jnp.max(sc, axis=0, keepdims=True))
    peak = m.astype(jnp.bfloat16).astype(jnp.float32)

    def second(s, tot):
        blk = picked_ref[item * MOST + s]
        start = pl.multiple_of(blk * BLK, BLK)
        vsel_ref[s] = v_ref[pl.ds(start, BLK), :]
        w = jnp.exp(sc_ref[s] - peak)
        w_ref[s] = w.astype(jnp.bfloat16)
        return tot + jnp.sum(w, axis=0, keepdims=True)

    tot = lax.fori_loop(0, n, second, jnp.zeros((1, rows), jnp.float32))

    def blank(s, carry):
        vsel_ref[s] = jnp.zeros((BLK, HD), jnp.bfloat16)
        w_ref[s] = jnp.zeros((BLK, rows), jnp.bfloat16)
        return carry

    lax.fori_loop(n, MOST, blank, 0)
    acc = lax.dot_general(
        vsel_ref[...].reshape(MOST * BLK, HD), w_ref[...].reshape(MOST * BLK, rows),
        (((0,), (0,)), ((), ())), preferred_element_type=jnp.float32,
    )
    total = tot.astype(jnp.bfloat16).astype(jnp.float32)
    out = (acc / total).astype(jnp.bfloat16)
    extra = part_ref.shape[3] - HD
    slab_rows = lax.broadcasted_iota(jnp.int32, (extra, rows), 0)
    slab = jnp.where(slab_rows == 0, peak, jnp.where(slab_rows == 1, total, 0.0))
    slab = slab.astype(jnp.bfloat16)
    chunks = part_ref.shape[1]
    width = rows // chunks
    for j in range(chunks):
        part_ref[0, j, 0, 0:HD, :] = out[:, j * width:(j + 1) * width]
        part_ref[0, j, 0, HD:, :] = slab[:, j * width:(j + 1) * width]


def on_device(queries, key_cache, value_cache, blocks, out_weight):
    shard_count = lax.axis_size("ctx")
    here_index = lax.axis_index("ctx")
    local_heads = key_cache.shape[1] // HD
    tq = queries.shape[0]
    group_size = queries.shape[1] // (local_heads * HD)
    blocks_here = key_cache.shape[0] // BLK
    query_tokens = tq * shard_count
    qblocks = query_tokens // BLK
    per_block = shard_count // qblocks
    rows = group_size * BLK
    width = rows // per_block
    extra = 16
    total_keys = shard_count * key_cache.shape[0]

    block_lists = lax.dynamic_slice_in_dim(
        blocks, lax.axis_index("kv") * local_heads, local_heads, 1
    )
    shard_first = here_index * blocks_here
    picked, inside = block_tables(block_lists, shard_first, blocks_here)
    pos0 = (shard_first * BLK - (total_keys - query_tokens)).astype(jnp.int32).reshape(1)

    qt = queries.reshape(tq, local_heads * group_size, HD).transpose(1, 0, 2)
    tables = (picked.reshape(-1).astype(jnp.int32), inside.reshape(-1).astype(jnp.int32), pos0)
    q_all, tables = gather_ctx(qt, tables)
    q_all = q_all.reshape(qblocks, per_block, local_heads, group_size, tq, HD)

    kernel = functools.partial(
        attn_kernel, heads=local_heads, rows=rows, tq=tq, score_scale=1.0 / math.sqrt(HD)
    )
    grid_spec = pltpu.PrefetchScalarGridSpec(
        num_scalar_prefetch=3,
        grid=(local_heads, qblocks),
        in_specs=[
            pl.BlockSpec((1, per_block, 1, group_size, tq, HD),
                         lambda h, b, *_: (b, 0, h, 0, 0, 0)),
            pl.BlockSpec((key_cache.shape[0], HD), lambda h, b, *_: (0, h)),
            pl.BlockSpec((value_cache.shape[0], HD), lambda h, b, *_: (0, h)),
        ],
        out_specs=pl.BlockSpec((1, per_block, 1, HD + extra, width),
                               lambda h, b, *_: (b, 0, h, 0, 0)),
        scratch_shapes=[
            pltpu.VMEM((MOST, BLK, rows), jnp.float32),
            pltpu.VMEM((MOST, BLK, HD), jnp.bfloat16),
            pltpu.VMEM((MOST, BLK, rows), jnp.bfloat16),
        ],
    )
    part = pl.pallas_call(
        kernel,
        grid_spec=grid_spec,
        out_shape=jax.ShapeDtypeStruct(
            (qblocks, per_block, local_heads, HD + extra, width), jnp.bfloat16
        ),
        compiler_params=pltpu.CompilerParams(
            dimension_semantics=("arbitrary", "arbitrary"),
        ),
    )(*tables, q_all, key_cache, value_cache)

    part = part.reshape(shard_count, local_heads, HD + extra, width)
    part_in = lax.all_to_all(part, "ctx", 0, 0, tiled=True).astype(jnp.float32)
    peak_all = part_in[:, :, HD, :]
    peak_top = jnp.max(peak_all, axis=0)
    weight_all = part_in[:, :, HD + 1, :] * jnp.exp(peak_all - peak_top)
    summed = jnp.sum(weight_all[:, :, None, :] * part_in[:, :, :HD, :], axis=0)
    merged = summed / jnp.sum(weight_all, axis=0)[:, None, :]
    merged = merged.reshape(local_heads, HD, group_size, tq).transpose(3, 0, 2, 1)
    attended_heads = merged.astype(jnp.bfloat16).reshape(tq, -1)
    projected = jnp.dot(
        gather_ctx(attended_heads).reshape(-1, attended_heads.shape[1]),
        out_weight,
        preferred_element_type=jnp.float32,
    )
    return reduce_kv(projected).astype(jnp.bfloat16)


def solution(mesh):
    placed = (P("ctx", "kv"), P("ctx", "kv"), P("ctx", "kv"), P(), P("kv", "ctx"))
    return jax.shard_map(
        on_device, mesh=mesh, in_specs=placed, out_specs=P("kv", "ctx"), check_vma=False
    )
```

```python
import functools
import math

import jax
import jax.numpy as jnp
from jax import lax
from jax.experimental import pallas as pl
from jax.experimental.pallas import tpu as pltpu
from jax.sharding import PartitionSpec as P

HD = 128
BLK = 128
MOST = 7

ORDERS = ((8, 4, 32, 16, 2), (32, 8, 4, 2, 16))


def gather_ctx(x, tie=None):
    n = lax.axis_size("ctx")
    me = lax.axis_index("ctx")
    core = me % 2
    steps = len(ORDERS[0])
    buf = x[None]
    for step in range(steps):
        a0, a1 = ORDERS[0][step], ORDERS[1][step]
        pairs = [(c, c ^ (a0 if c % 2 == 0 else a1)) for c in range(n)]
        other = lax.ppermute(buf, "ctx", pairs)
        low = (me & jnp.where(core == 0, a0, a1)) == 0
        buf = jnp.where(low, jnp.concatenate([buf, other]), jnp.concatenate([other, buf]))
        if step == 0 and tie is not None:
            buf, tie = lax.optimization_barrier((buf, tie))
    tail = buf.shape[1:]
    outs = []
    for order in ORDERS:
        dims_bits = [order[steps - 1 - d].bit_length() - 2 for d in range(steps)]
        perm = [dims_bits.index(bb) for bb in reversed(range(steps))]
        t = buf.reshape((2,) * steps + tail)
        t = t.transpose(perm + list(range(steps, steps + len(tail))))
        outs.append(t.reshape((2 ** steps,) + tail))
    mine = jnp.where(core == 0, outs[0], outs[1])
    other = lax.ppermute(mine, "ctx", [(c, c ^ 1) for c in range(n)])
    both = jnp.where(core == 0, jnp.stack([mine, other], 1), jnp.stack([other, mine], 1))
    if tie is None:
        return both.reshape((n,) + tail)
    return both.reshape((n,) + tail), tie


def reduce_kv(part):
    n = lax.axis_size("kv")
    me = lax.axis_index("kv")
    bit = n // 2
    while bit >= 1:
        half = part.shape[0] // 2
        high = (me & bit) != 0
        keep = jnp.where(high, part[half:], part[:half])
        send = jnp.where(high, part[:half], part[half:])
        part = keep + lax.ppermute(send, "kv", [(i, i ^ bit) for i in range(n)])
        bit //= 2
    return part


def block_tables(block_lists, shard_first, blocks_here):
    below = jnp.sum((block_lists < shard_first).astype(jnp.int32), axis=-1)
    inside = jnp.sum(
        ((block_lists >= shard_first) & (block_lists < shard_first + blocks_here)).astype(
            jnp.int32
        ),
        axis=-1,
    )
    slot_ids = jnp.arange(MOST, dtype=jnp.int32)
    places = jnp.clip(below[..., None] + slot_ids, 0, block_lists.shape[-1] - 1)
    picked = jnp.take_along_axis(block_lists, places, axis=-1) - shard_first
    usable = slot_ids < inside[..., None]
    picked = jnp.where(usable, picked, 0)
    return picked, inside


def attn_kernel(picked_ref, count_ref, pos_ref, q_ref, k_ref, v_ref, part_ref, sc_ref,
                vsel_ref, w_ref, *, heads, rows, tq, score_scale):
    b = pl.program_id(0)
    h = pl.program_id(1)
    item = b * heads + h
    n = count_ref[item]
    q_t = q_ref[...].reshape(rows, HD).astype(jnp.float32).T.astype(jnp.bfloat16)
    key_ids = lax.broadcasted_iota(jnp.int32, (BLK, rows), 0)
    row_ids = lax.broadcasted_iota(jnp.int32, (BLK, rows), 1)
    tok = (row_ids // (rows // (BLK // tq))) * tq + row_ids % tq
    limit = b * BLK + tok - pos_ref[0]

    def scores(s):
        blk = picked_ref[item * MOST + s]
        start = pl.multiple_of(blk * BLK, BLK)
        kb = k_ref[pl.ds(start, BLK), :]
        sc = jnp.dot(kb, q_t, preferred_element_type=jnp.float32)
        return blk, sc * score_scale

    def first(s, m):
        blk, sc = scores(s)
        sc_ref[s] = sc
        return jnp.maximum(m, jnp.max(sc, axis=0, keepdims=True))

    last = jnp.maximum(n - 1, 0)
    m = lax.fori_loop(0, last, first, jnp.full((1, rows), -jnp.inf, jnp.float32))
    blk, sc = scores(last)
    sc = jnp.where(blk * BLK + key_ids <= limit, sc, -jnp.inf)
    sc_ref[last] = sc
    m = jnp.maximum(m, jnp.max(sc, axis=0, keepdims=True))
    peak = m.astype(jnp.bfloat16).astype(jnp.float32)

    def second(s, tot):
        blk = picked_ref[item * MOST + s]
        start = pl.multiple_of(blk * BLK, BLK)
        vsel_ref[s] = v_ref[pl.ds(start, BLK), :]
        w = jnp.exp(sc_ref[s] - peak)
        w_ref[s] = w.astype(jnp.bfloat16)
        return tot + jnp.sum(w, axis=0, keepdims=True)

    tot = lax.fori_loop(0, n, second, jnp.zeros((1, rows), jnp.float32))

    def blank(s, carry):
        vsel_ref[s] = jnp.zeros((BLK, HD), jnp.bfloat16)
        w_ref[s] = jnp.zeros((BLK, rows), jnp.bfloat16)
        return carry

    lax.fori_loop(n, MOST, blank, 0)
    acc = lax.dot_general(
        vsel_ref[...].reshape(MOST * BLK, HD), w_ref[...].reshape(MOST * BLK, rows),
        (((0,), (0,)), ((), ())), preferred_element_type=jnp.float32,
    )
    total = tot.astype(jnp.bfloat16).astype(jnp.float32)
    out = (acc / total).astype(jnp.bfloat16)
    slab = jnp.concatenate([peak, total], axis=0).astype(jnp.bfloat16)
    chunks = part_ref.shape[1]
    width = rows // chunks
    for head in range(heads):
        @pl.when(h == head)
        def _():
            for j in range(chunks):
                part_ref[0, j, head * HD:(head + 1) * HD, :] = out[:, j * width:(j + 1) * width]
                part_ref[0, j, heads * HD + 2 * head:heads * HD + 2 * head + 2, :] = (
                    slab[:, j * width:(j + 1) * width]
                )


def on_device(queries, key_cache, value_cache, blocks, out_weight):
    shard_count = lax.axis_size("ctx")
    here_index = lax.axis_index("ctx")
    local_heads = key_cache.shape[1] // HD
    tq = queries.shape[0]
    group_size = queries.shape[1] // (local_heads * HD)
    blocks_here = key_cache.shape[0] // BLK
    query_tokens = tq * shard_count
    qblocks = query_tokens // BLK
    per_block = shard_count // qblocks
    rows = group_size * BLK
    width = rows // per_block
    slab_rows = local_heads * HD + 16
    total_keys = shard_count * key_cache.shape[0]

    block_lists = lax.dynamic_slice_in_dim(
        blocks, lax.axis_index("kv") * local_heads, local_heads, 1
    )
    shard_first = here_index * blocks_here
    picked, inside = block_tables(block_lists, shard_first, blocks_here)
    pos0 = (shard_first * BLK - (total_keys - query_tokens)).astype(jnp.int32).reshape(1)

    qt = queries.reshape(tq, local_heads * group_size, HD).transpose(1, 0, 2)
    tables = (picked.reshape(-1).astype(jnp.int32), inside.reshape(-1).astype(jnp.int32), pos0)
    q_all, tables = gather_ctx(qt, tables)
    q_all = q_all.reshape(qblocks, per_block, local_heads, group_size, tq, HD)

    kernel = functools.partial(
        attn_kernel, heads=local_heads, rows=rows, tq=tq, score_scale=1.0 / math.sqrt(HD)
    )
    grid_spec = pltpu.PrefetchScalarGridSpec(
        num_scalar_prefetch=3,
        grid=(qblocks, local_heads),
        in_specs=[
            pl.BlockSpec((1, per_block, 1, group_size, tq, HD),
                         lambda b, h, *_: (b, 0, h, 0, 0, 0)),
            pl.BlockSpec((key_cache.shape[0], HD), lambda b, h, *_: (0, h)),
            pl.BlockSpec((value_cache.shape[0], HD), lambda b, h, *_: (0, h)),
        ],
        out_specs=pl.BlockSpec((1, per_block, slab_rows, width),
                               lambda b, h, *_: (b, 0, 0, 0)),
        scratch_shapes=[
            pltpu.VMEM((MOST, BLK, rows), jnp.float32),
            pltpu.VMEM((MOST, BLK, HD), jnp.bfloat16),
            pltpu.VMEM((MOST, BLK, rows), jnp.bfloat16),
        ],
    )
    part = pl.pallas_call(
        kernel,
        grid_spec=grid_spec,
        out_shape=jax.ShapeDtypeStruct((qblocks, per_block, slab_rows, width), jnp.bfloat16),
        compiler_params=pltpu.CompilerParams(
            dimension_semantics=("arbitrary", "arbitrary"),
        ),
    )(*tables, q_all, key_cache, value_cache)

    part = part.reshape(shard_count, slab_rows, width)
    part_in = lax.all_to_all(part, "ctx", 0, 0, tiled=True).astype(jnp.float32)
    stats = part_in[:, local_heads * HD:local_heads * HD + 2 * local_heads, :]
    stats = stats.reshape(shard_count, local_heads, 2, width)
    peak_all = stats[:, :, 0, :]
    peak_top = jnp.max(peak_all, axis=0)
    weight_all = stats[:, :, 1, :] * jnp.exp(peak_all - peak_top)
    values_in = part_in[:, :local_heads * HD, :].reshape(shard_count, local_heads, HD, width)
    summed = jnp.sum(weight_all[:, :, None, :] * values_in, axis=0)
    merged = summed / jnp.sum(weight_all, axis=0)[:, None, :]
    merged = merged.reshape(local_heads, HD, group_size, tq).transpose(3, 0, 2, 1)
    attended_heads = merged.astype(jnp.bfloat16).reshape(tq, -1)
    projected = jnp.dot(
        gather_ctx(attended_heads).reshape(-1, attended_heads.shape[1]),
        out_weight,
        preferred_element_type=jnp.float32,
    )
    return reduce_kv(projected).astype(jnp.bfloat16)


def solution(mesh):
    placed = (P("ctx", "kv"), P("ctx", "kv"), P("ctx", "kv"), P(), P("kv", "ctx"))
    return jax.shard_map(
        on_device, mesh=mesh, in_specs=placed, out_specs=P("kv", "ctx"), check_vma=False
    )
```

```python
import functools
import math

import jax
import jax.numpy as jnp
from jax import lax
from jax.experimental import pallas as pl
from jax.experimental.pallas import tpu as pltpu
from jax.sharding import PartitionSpec as P

HD = 128
BLK = 128
MOST = 7

ORDERS = ((8, 4, 32, 16, 2), (32, 8, 4, 2, 16))


def gather_ctx(x, tie=None, halves=False):
    n = lax.axis_size("ctx")
    me = lax.axis_index("ctx")
    core = me % 2
    steps = len(ORDERS[0])
    buf = x[None]
    for step in range(steps):
        a0, a1 = ORDERS[0][step], ORDERS[1][step]
        pairs = [(c, c ^ (a0 if c % 2 == 0 else a1)) for c in range(n)]
        other = lax.ppermute(buf, "ctx", pairs)
        low = (me & jnp.where(core == 0, a0, a1)) == 0
        buf = jnp.where(low, jnp.concatenate([buf, other]), jnp.concatenate([other, buf]))
        if step == 0 and tie is not None:
            buf, tie = lax.optimization_barrier((buf, tie))
    tail = buf.shape[1:]
    outs = []
    for order in ORDERS:
        dims_bits = [order[steps - 1 - d].bit_length() - 2 for d in range(steps)]
        perm = [dims_bits.index(bb) for bb in reversed(range(steps))]
        t = buf.reshape((2,) * steps + tail)
        t = t.transpose(perm + list(range(steps, steps + len(tail))))
        outs.append(t.reshape((2 ** steps,) + tail))
    mine = jnp.where(core == 0, outs[0], outs[1])
    other = lax.ppermute(mine, "ctx", [(c, c ^ 1) for c in range(n)])
    if halves:
        return mine, other
    both = jnp.where(core == 0, jnp.stack([mine, other], 1), jnp.stack([other, mine], 1))
    if tie is None:
        return both.reshape((n,) + tail)
    return both.reshape((n,) + tail), tie


def reduce_kv(part):
    n = lax.axis_size("kv")
    me = lax.axis_index("kv")
    bit = n // 2
    while bit >= 1:
        half = part.shape[0] // 2
        high = (me & bit) != 0
        keep = jnp.where(high, part[half:], part[:half])
        send = jnp.where(high, part[:half], part[half:])
        part = keep + lax.ppermute(send, "kv", [(i, i ^ bit) for i in range(n)])
        bit //= 2
    return part


def block_tables(block_lists, shard_first, blocks_here):
    below = jnp.sum((block_lists < shard_first).astype(jnp.int32), axis=-1)
    inside = jnp.sum(
        ((block_lists >= shard_first) & (block_lists < shard_first + blocks_here)).astype(
            jnp.int32
        ),
        axis=-1,
    )
    slot_ids = jnp.arange(MOST, dtype=jnp.int32)
    places = jnp.clip(below[..., None] + slot_ids, 0, block_lists.shape[-1] - 1)
    picked = jnp.take_along_axis(block_lists, places, axis=-1) - shard_first
    usable = slot_ids < inside[..., None]
    picked = jnp.where(usable, picked, 0)
    return picked, inside


def attn_kernel(picked_ref, count_ref, pos_ref, q_ref, k_ref, v_ref, part_ref, sc_ref,
                vsel_ref, w_ref, *, heads, rows, tq, score_scale):
    b = pl.program_id(0)
    h = pl.program_id(1)
    item = b * heads + h
    n = count_ref[item]
    q_t = q_ref[...].reshape(rows, HD).astype(jnp.float32).T.astype(jnp.bfloat16)
    key_ids = lax.broadcasted_iota(jnp.int32, (BLK, rows), 0)
    row_ids = lax.broadcasted_iota(jnp.int32, (BLK, rows), 1)
    tok = (row_ids // (rows // (BLK // tq))) * tq + row_ids % tq
    limit = b * BLK + tok - pos_ref[0]

    def scores(s):
        blk = picked_ref[item * MOST + s]
        start = pl.multiple_of(blk * BLK, BLK)
        kb = k_ref[pl.ds(start, BLK), :]
        sc = jnp.dot(kb, q_t, preferred_element_type=jnp.float32)
        return blk, sc * score_scale

    def first(s, m):
        blk, sc = scores(s)
        sc_ref[s] = sc
        return jnp.maximum(m, jnp.max(sc, axis=0, keepdims=True))

    last = jnp.maximum(n - 1, 0)
    m = lax.fori_loop(0, last, first, jnp.full((1, rows), -jnp.inf, jnp.float32))
    blk, sc = scores(last)
    sc = jnp.where(blk * BLK + key_ids <= limit, sc, -jnp.inf)
    sc_ref[last] = sc
    m = jnp.maximum(m, jnp.max(sc, axis=0, keepdims=True))
    peak = m.astype(jnp.bfloat16).astype(jnp.float32)

    def second(s, tot):
        blk = picked_ref[item * MOST + s]
        start = pl.multiple_of(blk * BLK, BLK)
        vsel_ref[s] = v_ref[pl.ds(start, BLK), :]
        w = jnp.exp(sc_ref[s] - peak)
        w_ref[s] = w.astype(jnp.bfloat16)
        return tot + jnp.sum(w, axis=0, keepdims=True)

    tot = lax.fori_loop(0, n, second, jnp.zeros((1, rows), jnp.float32))

    def blank(s, carry):
        vsel_ref[s] = jnp.zeros((BLK, HD), jnp.bfloat16)
        w_ref[s] = jnp.zeros((BLK, rows), jnp.bfloat16)
        return carry

    lax.fori_loop(n, MOST, blank, 0)
    acc = lax.dot_general(
        vsel_ref[...].reshape(MOST * BLK, HD), w_ref[...].reshape(MOST * BLK, rows),
        (((0,), (0,)), ((), ())), preferred_element_type=jnp.float32,
    )
    total = tot.astype(jnp.bfloat16).astype(jnp.float32)
    out = (acc / total).astype(jnp.bfloat16)
    slab = jnp.concatenate([peak, total], axis=0).astype(jnp.bfloat16)
    chunks = part_ref.shape[1]
    width = rows // chunks
    for head in range(heads):
        @pl.when(h == head)
        def _():
            for j in range(chunks):
                part_ref[0, j, head * HD:(head + 1) * HD, :] = out[:, j * width:(j + 1) * width]
                part_ref[0, j, heads * HD + 2 * head:heads * HD + 2 * head + 2, :] = (
                    slab[:, j * width:(j + 1) * width]
                )


def on_device(queries, key_cache, value_cache, blocks, out_weight):
    shard_count = lax.axis_size("ctx")
    here_index = lax.axis_index("ctx")
    local_heads = key_cache.shape[1] // HD
    tq = queries.shape[0]
    group_size = queries.shape[1] // (local_heads * HD)
    blocks_here = key_cache.shape[0] // BLK
    query_tokens = tq * shard_count
    qblocks = query_tokens // BLK
    per_block = shard_count // qblocks
    rows = group_size * BLK
    width = rows // per_block
    slab_rows = local_heads * HD + 16
    total_keys = shard_count * key_cache.shape[0]

    block_lists = lax.dynamic_slice_in_dim(
        blocks, lax.axis_index("kv") * local_heads, local_heads, 1
    )
    shard_first = here_index * blocks_here
    picked, inside = block_tables(block_lists, shard_first, blocks_here)
    pos0 = (shard_first * BLK - (total_keys - query_tokens)).astype(jnp.int32).reshape(1)

    qt = queries.reshape(tq, local_heads * group_size, HD).transpose(1, 0, 2)
    tables = (picked.reshape(-1).astype(jnp.int32), inside.reshape(-1).astype(jnp.int32), pos0)
    q_all, tables = gather_ctx(qt, tables)
    q_all = q_all.reshape(qblocks, per_block, local_heads, group_size, tq, HD)

    kernel = functools.partial(
        attn_kernel, heads=local_heads, rows=rows, tq=tq, score_scale=1.0 / math.sqrt(HD)
    )
    grid_spec = pltpu.PrefetchScalarGridSpec(
        num_scalar_prefetch=3,
        grid=(qblocks, local_heads),
        in_specs=[
            pl.BlockSpec((1, per_block, 1, group_size, tq, HD),
                         lambda b, h, *_: (b, 0, h, 0, 0, 0)),
            pl.BlockSpec((key_cache.shape[0], HD), lambda b, h, *_: (0, h)),
            pl.BlockSpec((value_cache.shape[0], HD), lambda b, h, *_: (0, h)),
        ],
        out_specs=pl.BlockSpec((1, per_block, slab_rows, width),
                               lambda b, h, *_: (b, 0, 0, 0)),
        scratch_shapes=[
            pltpu.VMEM((MOST, BLK, rows), jnp.float32),
            pltpu.VMEM((MOST, BLK, HD), jnp.bfloat16),
            pltpu.VMEM((MOST, BLK, rows), jnp.bfloat16),
        ],
    )
    part = pl.pallas_call(
        kernel,
        grid_spec=grid_spec,
        out_shape=jax.ShapeDtypeStruct((qblocks, per_block, slab_rows, width), jnp.bfloat16),
        compiler_params=pltpu.CompilerParams(
            dimension_semantics=("arbitrary", "arbitrary"),
        ),
    )(*tables, q_all, key_cache, value_cache)

    part = part.reshape(shard_count, slab_rows, width)
    part_in = lax.all_to_all(part, "ctx", 0, 0, tiled=True).astype(jnp.float32)
    stats = part_in[:, local_heads * HD:local_heads * HD + 2 * local_heads, :]
    stats = stats.reshape(shard_count, local_heads, 2, width)
    peak_all = stats[:, :, 0, :]
    peak_top = jnp.max(peak_all, axis=0)
    weight_all = stats[:, :, 1, :] * jnp.exp(peak_all - peak_top)
    values_in = part_in[:, :local_heads * HD, :].reshape(shard_count, local_heads, HD, width)
    summed = jnp.sum(weight_all[:, :, None, :] * values_in, axis=0)
    merged = summed / jnp.sum(weight_all, axis=0)[:, None, :]
    merged = merged.reshape(local_heads, HD, group_size, tq).transpose(3, 0, 2, 1)
    attended_heads = merged.astype(jnp.bfloat16).reshape(tq, -1)
    mine, other = gather_ctx(attended_heads, halves=True)
    core = here_index % 2
    mine, other = (
        jnp.dot(part.reshape(-1, attended_heads.shape[1]), out_weight,
                preferred_element_type=jnp.float32).reshape(shard_count // 2, tq, -1)
        for part in (mine, other)
    )
    projected = jnp.where(
        core == 0, jnp.stack([mine, other], 1), jnp.stack([other, mine], 1)
    ).reshape(query_tokens, -1)
    return reduce_kv(projected).astype(jnp.bfloat16)


def solution(mesh):
    placed = (P("ctx", "kv"), P("ctx", "kv"), P("ctx", "kv"), P(), P("kv", "ctx"))
    return jax.shard_map(
        on_device, mesh=mesh, in_specs=placed, out_specs=P("kv", "ctx"), check_vma=False
    )
```

```python
import functools
import math

import jax
import jax.numpy as jnp
from jax import lax
from jax.experimental import pallas as pl
from jax.experimental.pallas import tpu as pltpu
from jax.sharding import PartitionSpec as P

HD = 128
BLK = 128
MOST = 7

ORDERS = ((8, 4, 32, 16, 2), (32, 8, 4, 2, 16))


def gather_ctx(x, tie=None, halves=False):
    n = lax.axis_size("ctx")
    me = lax.axis_index("ctx")
    core = me % 2
    steps = len(ORDERS[0])
    buf = x[None]
    for step in range(steps):
        a0, a1 = ORDERS[0][step], ORDERS[1][step]
        pairs = [(c, c ^ (a0 if c % 2 == 0 else a1)) for c in range(n)]
        other = lax.ppermute(buf, "ctx", pairs)
        low = (me & jnp.where(core == 0, a0, a1)) == 0
        buf = jnp.where(low, jnp.concatenate([buf, other]), jnp.concatenate([other, buf]))
        if step == 0 and tie is not None:
            buf, tie = lax.optimization_barrier((buf, tie))
    tail = buf.shape[1:]
    outs = []
    for order in ORDERS:
        dims_bits = [order[steps - 1 - d].bit_length() - 2 for d in range(steps)]
        perm = [dims_bits.index(bb) for bb in reversed(range(steps))]
        t = buf.reshape((2,) * steps + tail)
        t = t.transpose(perm + list(range(steps, steps + len(tail))))
        outs.append(t.reshape((2 ** steps,) + tail))
    mine = jnp.where(core == 0, outs[0], outs[1])
    other = lax.ppermute(mine, "ctx", [(c, c ^ 1) for c in range(n)])
    if halves:
        result = (mine, other)
    else:
        both = jnp.where(core == 0, jnp.stack([mine, other], 1), jnp.stack([other, mine], 1))
        result = both.reshape((n,) + tail)
    return result if tie is None else (result, tie)


def reduce_kv(part):
    n = lax.axis_size("kv")
    me = lax.axis_index("kv")
    bit = n // 2
    while bit >= 1:
        half = part.shape[0] // 2
        high = (me & bit) != 0
        keep = jnp.where(high, part[half:], part[:half])
        send = jnp.where(high, part[:half], part[half:])
        part = keep + lax.ppermute(send, "kv", [(i, i ^ bit) for i in range(n)])
        bit //= 2
    return part


def block_tables(block_lists, shard_first, blocks_here):
    below = jnp.sum((block_lists < shard_first).astype(jnp.int32), axis=-1)
    inside = jnp.sum(
        ((block_lists >= shard_first) & (block_lists < shard_first + blocks_here)).astype(
            jnp.int32
        ),
        axis=-1,
    )
    slot_ids = jnp.arange(MOST, dtype=jnp.int32)
    places = jnp.clip(below[..., None] + slot_ids, 0, block_lists.shape[-1] - 1)
    picked = jnp.take_along_axis(block_lists, places, axis=-1) - shard_first
    usable = slot_ids < inside[..., None]
    picked = jnp.where(usable, picked, 0)
    return picked, inside


def attn_kernel(picked_ref, count_ref, pos_ref, qa_ref, qb_ref, k_ref, v_ref, part_ref, sc_ref,
                vsel_ref, w_ref, *, heads, rows, tq, score_scale):
    b = pl.program_id(0)
    h = pl.program_id(1)
    item = b * heads + h
    n = count_ref[item]
    core = pos_ref[1]
    q = jnp.stack([qa_ref[0, :, 0], qb_ref[0, :, 0]], axis=1).reshape(rows, HD)
    q_t = q.astype(jnp.float32).T.astype(jnp.bfloat16)
    key_ids = lax.broadcasted_iota(jnp.int32, (BLK, rows), 0)
    row_ids = lax.broadcasted_iota(jnp.int32, (BLK, rows), 1)
    tok = lax.bitwise_xor(row_ids // (rows // (BLK // tq)), core) * tq + row_ids % tq
    limit = b * BLK + tok - pos_ref[0]

    def scores(s):
        blk = picked_ref[item * MOST + s]
        start = pl.multiple_of(blk * BLK, BLK)
        kb = k_ref[pl.ds(start, BLK), :]
        sc = jnp.dot(kb, q_t, preferred_element_type=jnp.float32)
        return blk, sc * score_scale

    def first(s, m):
        blk, sc = scores(s)
        sc_ref[s] = sc
        return jnp.maximum(m, jnp.max(sc, axis=0, keepdims=True))

    last = jnp.maximum(n - 1, 0)
    m = lax.fori_loop(0, last, first, jnp.full((1, rows), -jnp.inf, jnp.float32))
    blk, sc = scores(last)
    sc = jnp.where(blk * BLK + key_ids <= limit, sc, -jnp.inf)
    sc_ref[last] = sc
    m = jnp.maximum(m, jnp.max(sc, axis=0, keepdims=True))
    peak = m.astype(jnp.bfloat16).astype(jnp.float32)

    def second(s, tot):
        blk = picked_ref[item * MOST + s]
        start = pl.multiple_of(blk * BLK, BLK)
        vsel_ref[s] = v_ref[pl.ds(start, BLK), :]
        w = jnp.exp(sc_ref[s] - peak)
        w_ref[s] = w.astype(jnp.bfloat16)
        return tot + jnp.sum(w, axis=0, keepdims=True)

    tot = lax.fori_loop(0, n, second, jnp.zeros((1, rows), jnp.float32))

    def blank(s, carry):
        vsel_ref[s] = jnp.zeros((BLK, HD), jnp.bfloat16)
        w_ref[s] = jnp.zeros((BLK, rows), jnp.bfloat16)
        return carry

    lax.fori_loop(n, MOST, blank, 0)
    acc = lax.dot_general(
        vsel_ref[...].reshape(MOST * BLK, HD), w_ref[...].reshape(MOST * BLK, rows),
        (((0,), (0,)), ((), ())), preferred_element_type=jnp.float32,
    )
    total = tot.astype(jnp.bfloat16).astype(jnp.float32)
    out = (acc / total).astype(jnp.bfloat16)
    slab = jnp.concatenate([peak, total], axis=0).astype(jnp.bfloat16)
    chunks = part_ref.shape[1]
    width = rows // chunks
    for head in range(heads):
        @pl.when(h == head)
        def _():
            for j in range(chunks):
                jj = lax.bitwise_xor(j, core)
                part_ref[0, jj, head * HD:(head + 1) * HD, :] = out[:, j * width:(j + 1) * width]
                part_ref[0, jj, heads * HD + 2 * head:heads * HD + 2 * head + 2, :] = (
                    slab[:, j * width:(j + 1) * width]
                )


def on_device(queries, key_cache, value_cache, blocks, out_weight):
    shard_count = lax.axis_size("ctx")
    here_index = lax.axis_index("ctx")
    local_heads = key_cache.shape[1] // HD
    tq = queries.shape[0]
    group_size = queries.shape[1] // (local_heads * HD)
    blocks_here = key_cache.shape[0] // BLK
    query_tokens = tq * shard_count
    qblocks = query_tokens // BLK
    per_block = shard_count // qblocks
    rows = group_size * BLK
    width = rows // per_block
    slab_rows = local_heads * HD + 16
    total_keys = shard_count * key_cache.shape[0]

    block_lists = lax.dynamic_slice_in_dim(
        blocks, lax.axis_index("kv") * local_heads, local_heads, 1
    )
    shard_first = here_index * blocks_here
    picked, inside = block_tables(block_lists, shard_first, blocks_here)
    pos0 = jnp.stack([
        (shard_first * BLK - (total_keys - query_tokens)).astype(jnp.int32),
        (here_index % 2).astype(jnp.int32),
    ])

    qt = queries.reshape(tq, local_heads * group_size, HD).transpose(1, 0, 2)
    tables = (picked.reshape(-1).astype(jnp.int32), inside.reshape(-1).astype(jnp.int32), pos0)
    (q_own, q_mate), tables = gather_ctx(qt, tables, halves=True)
    q_own = q_own.reshape(qblocks, per_block // 2, local_heads, group_size, tq, HD)
    q_mate = q_mate.reshape(qblocks, per_block // 2, local_heads, group_size, tq, HD)

    kernel = functools.partial(
        attn_kernel, heads=local_heads, rows=rows, tq=tq, score_scale=1.0 / math.sqrt(HD)
    )
    grid_spec = pltpu.PrefetchScalarGridSpec(
        num_scalar_prefetch=3,
        grid=(qblocks, local_heads),
        in_specs=[
            pl.BlockSpec((1, per_block // 2, 1, group_size, tq, HD),
                         lambda b, h, *_: (b, 0, h, 0, 0, 0)),
            pl.BlockSpec((1, per_block // 2, 1, group_size, tq, HD),
                         lambda b, h, *_: (b, 0, h, 0, 0, 0)),
            pl.BlockSpec((key_cache.shape[0], HD), lambda b, h, *_: (0, h)),
            pl.BlockSpec((value_cache.shape[0], HD), lambda b, h, *_: (0, h)),
        ],
        out_specs=pl.BlockSpec((1, per_block, slab_rows, width),
                               lambda b, h, *_: (b, 0, 0, 0)),
        scratch_shapes=[
            pltpu.VMEM((MOST, BLK, rows), jnp.float32),
            pltpu.VMEM((MOST, BLK, HD), jnp.bfloat16),
            pltpu.VMEM((MOST, BLK, rows), jnp.bfloat16),
        ],
    )
    part = pl.pallas_call(
        kernel,
        grid_spec=grid_spec,
        out_shape=jax.ShapeDtypeStruct((qblocks, per_block, slab_rows, width), jnp.bfloat16),
        compiler_params=pltpu.CompilerParams(
            dimension_semantics=("arbitrary", "arbitrary"),
        ),
    )(*tables, q_own, q_mate, key_cache, value_cache)

    part = part.reshape(shard_count, slab_rows, width)
    part_in = lax.all_to_all(part, "ctx", 0, 0, tiled=True).astype(jnp.float32)
    stats = part_in[:, local_heads * HD:local_heads * HD + 2 * local_heads, :]
    stats = stats.reshape(shard_count, local_heads, 2, width)
    peak_all = stats[:, :, 0, :]
    peak_top = jnp.max(peak_all, axis=0)
    weight_all = stats[:, :, 1, :] * jnp.exp(peak_all - peak_top)
    values_in = part_in[:, :local_heads * HD, :].reshape(shard_count, local_heads, HD, width)
    summed = jnp.sum(weight_all[:, :, None, :] * values_in, axis=0)
    merged = summed / jnp.sum(weight_all, axis=0)[:, None, :]
    merged = merged.reshape(local_heads, HD, group_size, tq).transpose(3, 0, 2, 1)
    attended_heads = merged.astype(jnp.bfloat16).reshape(tq, -1)
    mine, other = gather_ctx(attended_heads, halves=True)
    core = here_index % 2
    mine, other = (
        jnp.dot(part.reshape(-1, attended_heads.shape[1]), out_weight,
                preferred_element_type=jnp.float32).reshape(shard_count // 2, tq, -1)
        for part in (mine, other)
    )
    projected = jnp.where(
        core == 0, jnp.stack([mine, other], 1), jnp.stack([other, mine], 1)
    ).reshape(query_tokens, -1)
    return reduce_kv(projected).astype(jnp.bfloat16)


def solution(mesh):
    placed = (P("ctx", "kv"), P("ctx", "kv"), P("ctx", "kv"), P(), P("kv", "ctx"))
    return jax.shard_map(
        on_device, mesh=mesh, in_specs=placed, out_specs=P("kv", "ctx"), check_vma=False
    )
```

```python
import functools
import math

import jax
import jax.numpy as jnp
from jax import lax
from jax.experimental import pallas as pl
from jax.experimental.pallas import tpu as pltpu
from jax.sharding import PartitionSpec as P

HD = 128
BLK = 128
MOST = 7

ORDERS = ((8, 4, 32, 16, 2), (32, 8, 4, 2, 16))


def gather_ctx(x, tie=None, halves=False):
    n = lax.axis_size("ctx")
    me = lax.axis_index("ctx")
    core = me % 2
    steps = len(ORDERS[0])
    buf = x[None]
    for step in range(steps):
        a0, a1 = ORDERS[0][step], ORDERS[1][step]
        pairs = [(c, c ^ (a0 if c % 2 == 0 else a1)) for c in range(n)]
        other = lax.ppermute(buf, "ctx", pairs)
        low = (me & jnp.where(core == 0, a0, a1)) == 0
        buf = jnp.where(low, jnp.concatenate([buf, other]), jnp.concatenate([other, buf]))
        if step == 0 and tie is not None:
            buf, tie = lax.optimization_barrier((buf, tie))
    tail = buf.shape[1:]
    outs = []
    for order in ORDERS:
        dims_bits = [order[steps - 1 - d].bit_length() - 2 for d in range(steps)]
        perm = [dims_bits.index(bb) for bb in reversed(range(steps))]
        t = buf.reshape((2,) * steps + tail)
        t = t.transpose(perm + list(range(steps, steps + len(tail))))
        outs.append(t.reshape((2 ** steps,) + tail))
    mine = jnp.where(core == 0, outs[0], outs[1])
    other = lax.ppermute(mine, "ctx", [(c, c ^ 1) for c in range(n)])
    if halves:
        return mine, other
    both = jnp.where(core == 0, jnp.stack([mine, other], 1), jnp.stack([other, mine], 1))
    if tie is None:
        return both.reshape((n,) + tail)
    return both.reshape((n,) + tail), tie


def reduce_kv(part):
    n = lax.axis_size("kv")
    me = lax.axis_index("kv")
    bits = n.bit_length() - 1
    part = part.reshape((2,) * bits + (part.shape[0] // n,) + part.shape[1:])
    for level in range(bits):
        axis = bits - 1 - level
        bit = 1 << level
        high = (me & bit) != 0
        lo = lax.index_in_dim(part, 0, axis, keepdims=False)
        hi = lax.index_in_dim(part, 1, axis, keepdims=False)
        keep = jnp.where(high, hi, lo)
        send = jnp.where(high, lo, hi)
        part = keep + lax.ppermute(send, "kv", [(i, i ^ bit) for i in range(n)])
    return part


def block_tables(block_lists, shard_first, blocks_here):
    below = jnp.sum((block_lists < shard_first).astype(jnp.int32), axis=-1)
    inside = jnp.sum(
        ((block_lists >= shard_first) & (block_lists < shard_first + blocks_here)).astype(
            jnp.int32
        ),
        axis=-1,
    )
    slot_ids = jnp.arange(MOST, dtype=jnp.int32)
    places = jnp.clip(below[..., None] + slot_ids, 0, block_lists.shape[-1] - 1)
    picked = jnp.take_along_axis(block_lists, places, axis=-1) - shard_first
    usable = slot_ids < inside[..., None]
    picked = jnp.where(usable, picked, 0)
    return picked, inside


def attn_kernel(picked_ref, count_ref, pos_ref, q_ref, k_ref, v_ref, part_ref, sc_ref,
                vsel_ref, w_ref, *, heads, rows, tq, score_scale):
    b = pl.program_id(0)
    h = pl.program_id(1)
    item = b * heads + h
    n = count_ref[item]
    q_t = q_ref[...].reshape(rows, HD).astype(jnp.float32).T.astype(jnp.bfloat16)
    key_ids = lax.broadcasted_iota(jnp.int32, (BLK, rows), 0)
    row_ids = lax.broadcasted_iota(jnp.int32, (BLK, rows), 1)
    tok = (row_ids // (rows // (BLK // tq))) * tq + row_ids % tq
    limit = b * BLK + tok - pos_ref[0]

    def scores(s):
        blk = picked_ref[item * MOST + s]
        start = pl.multiple_of(blk * BLK, BLK)
        kb = k_ref[pl.ds(start, BLK), :]
        sc = jnp.dot(kb, q_t, preferred_element_type=jnp.float32)
        return blk, sc * score_scale

    def first(s, m):
        blk, sc = scores(s)
        sc_ref[s] = sc
        return jnp.maximum(m, jnp.max(sc, axis=0, keepdims=True))

    last = jnp.maximum(n - 1, 0)
    m = lax.fori_loop(0, last, first, jnp.full((1, rows), -jnp.inf, jnp.float32))
    blk, sc = scores(last)
    sc = jnp.where(blk * BLK + key_ids <= limit, sc, -jnp.inf)
    sc_ref[last] = sc
    m = jnp.maximum(m, jnp.max(sc, axis=0, keepdims=True))
    peak = m.astype(jnp.bfloat16).astype(jnp.float32)

    def second(s, tot):
        blk = picked_ref[item * MOST + s]
        start = pl.multiple_of(blk * BLK, BLK)
        vsel_ref[s] = v_ref[pl.ds(start, BLK), :]
        w = jnp.exp(sc_ref[s] - peak)
        w_ref[s] = w.astype(jnp.bfloat16)
        return tot + jnp.sum(w, axis=0, keepdims=True)

    tot = lax.fori_loop(0, n, second, jnp.zeros((1, rows), jnp.float32))

    def blank(s, carry):
        vsel_ref[s] = jnp.zeros((BLK, HD), jnp.bfloat16)
        w_ref[s] = jnp.zeros((BLK, rows), jnp.bfloat16)
        return carry

    lax.fori_loop(n, MOST, blank, 0)
    acc = lax.dot_general(
        vsel_ref[...].reshape(MOST * BLK, HD), w_ref[...].reshape(MOST * BLK, rows),
        (((0,), (0,)), ((), ())), preferred_element_type=jnp.float32,
    )
    total = tot.astype(jnp.bfloat16).astype(jnp.float32)
    out = (acc / total).astype(jnp.bfloat16)
    slab = jnp.concatenate([peak, total], axis=0).astype(jnp.bfloat16)
    chunks = part_ref.shape[1]
    width = rows // chunks
    for head in range(heads):
        @pl.when(h == head)
        def _():
            for j in range(chunks):
                part_ref[0, j, head * HD:(head + 1) * HD, :] = out[:, j * width:(j + 1) * width]
                part_ref[0, j, heads * HD + 2 * head:heads * HD + 2 * head + 2, :] = (
                    slab[:, j * width:(j + 1) * width]
                )


def on_device(queries, key_cache, value_cache, blocks, out_weight):
    shard_count = lax.axis_size("ctx")
    here_index = lax.axis_index("ctx")
    local_heads = key_cache.shape[1] // HD
    tq = queries.shape[0]
    group_size = queries.shape[1] // (local_heads * HD)
    blocks_here = key_cache.shape[0] // BLK
    query_tokens = tq * shard_count
    qblocks = query_tokens // BLK
    per_block = shard_count // qblocks
    rows = group_size * BLK
    width = rows // per_block
    slab_rows = local_heads * HD + 16
    total_keys = shard_count * key_cache.shape[0]

    block_lists = lax.dynamic_slice_in_dim(
        blocks, lax.axis_index("kv") * local_heads, local_heads, 1
    )
    shard_first = here_index * blocks_here
    picked, inside = block_tables(block_lists, shard_first, blocks_here)
    pos0 = (shard_first * BLK - (total_keys - query_tokens)).astype(jnp.int32).reshape(1)

    qt = queries.reshape(tq, local_heads * group_size, HD).transpose(1, 0, 2)
    tables = (picked.reshape(-1).astype(jnp.int32), inside.reshape(-1).astype(jnp.int32), pos0)
    q_all, tables = gather_ctx(qt, tables)
    q_all = q_all.reshape(qblocks, per_block, local_heads, group_size, tq, HD)

    kernel = functools.partial(
        attn_kernel, heads=local_heads, rows=rows, tq=tq, score_scale=1.0 / math.sqrt(HD)
    )
    grid_spec = pltpu.PrefetchScalarGridSpec(
        num_scalar_prefetch=3,
        grid=(qblocks, local_heads),
        in_specs=[
            pl.BlockSpec((1, per_block, 1, group_size, tq, HD),
                         lambda b, h, *_: (b, 0, h, 0, 0, 0)),
            pl.BlockSpec((key_cache.shape[0], HD), lambda b, h, *_: (0, h)),
            pl.BlockSpec((value_cache.shape[0], HD), lambda b, h, *_: (0, h)),
        ],
        out_specs=pl.BlockSpec((1, per_block, slab_rows, width),
                               lambda b, h, *_: (b, 0, 0, 0)),
        scratch_shapes=[
            pltpu.VMEM((MOST, BLK, rows), jnp.float32),
            pltpu.VMEM((MOST, BLK, HD), jnp.bfloat16),
            pltpu.VMEM((MOST, BLK, rows), jnp.bfloat16),
        ],
    )
    part = pl.pallas_call(
        kernel,
        grid_spec=grid_spec,
        out_shape=jax.ShapeDtypeStruct((qblocks, per_block, slab_rows, width), jnp.bfloat16),
        compiler_params=pltpu.CompilerParams(
            dimension_semantics=("arbitrary", "arbitrary"),
        ),
    )(*tables, q_all, key_cache, value_cache)

    part = part.reshape(shard_count, slab_rows, width)
    part_in = lax.all_to_all(part, "ctx", 0, 0, tiled=True).astype(jnp.float32)
    stats = part_in[:, local_heads * HD:local_heads * HD + 2 * local_heads, :]
    stats = stats.reshape(shard_count, local_heads, 2, width)
    peak_all = stats[:, :, 0, :]
    peak_top = jnp.max(peak_all, axis=0)
    weight_all = stats[:, :, 1, :] * jnp.exp(peak_all - peak_top)
    values_in = part_in[:, :local_heads * HD, :].reshape(shard_count, local_heads, HD, width)
    summed = jnp.sum(weight_all[:, :, None, :] * values_in, axis=0)
    merged = summed / jnp.sum(weight_all, axis=0)[:, None, :]
    merged = merged.reshape(local_heads, HD, group_size, tq).transpose(3, 0, 2, 1)
    attended_heads = merged.astype(jnp.bfloat16).reshape(tq, -1)
    mine, other = gather_ctx(attended_heads, halves=True)
    core = here_index % 2
    mine, other = (
        jnp.dot(part.reshape(-1, attended_heads.shape[1]), out_weight,
                preferred_element_type=jnp.float32).reshape(shard_count // 2, tq, -1)
        for part in (mine, other)
    )
    projected = jnp.where(
        core == 0, jnp.stack([mine, other], 1), jnp.stack([other, mine], 1)
    ).reshape(query_tokens, -1)
    return reduce_kv(projected).astype(jnp.bfloat16)


def solution(mesh):
    placed = (P("ctx", "kv"), P("ctx", "kv"), P("ctx", "kv"), P(), P("kv", "ctx"))
    return jax.shard_map(
        on_device, mesh=mesh, in_specs=placed, out_specs=P("kv", "ctx"), check_vma=False
    )
```

```python
import functools
import math

import jax
import jax.numpy as jnp
from jax import lax
from jax.experimental import pallas as pl
from jax.experimental.pallas import tpu as pltpu
from jax.sharding import PartitionSpec as P

HD = 128
BLK = 128
MOST = 7

ORDERS = ((8, 4, 32, 16, 2), (32, 8, 4, 2, 16))


def gather_ctx(x, tie=None, halves=False):
    n = lax.axis_size("ctx")
    me = lax.axis_index("ctx")
    core = me % 2
    steps = len(ORDERS[0])
    buf = x[None]
    for step in range(steps):
        a0, a1 = ORDERS[0][step], ORDERS[1][step]
        pairs = [(c, c ^ (a0 if c % 2 == 0 else a1)) for c in range(n)]
        other = lax.ppermute(buf, "ctx", pairs)
        low = (me & jnp.where(core == 0, a0, a1)) == 0
        buf = jnp.where(low, jnp.concatenate([buf, other]), jnp.concatenate([other, buf]))
        if step == 0 and tie is not None:
            buf, tie = lax.optimization_barrier((buf, tie))
    tail = buf.shape[1:]
    outs = []
    for order in ORDERS:
        dims_bits = [order[steps - 1 - d].bit_length() - 2 for d in range(steps)]
        perm = [dims_bits.index(bb) for bb in reversed(range(steps))]
        t = buf.reshape((2,) * steps + tail)
        t = t.transpose(perm + list(range(steps, steps + len(tail))))
        outs.append(t.reshape((2 ** steps,) + tail))
    mine = jnp.where(core == 0, outs[0], outs[1])
    other = lax.ppermute(mine, "ctx", [(c, c ^ 1) for c in range(n)])
    if halves:
        return mine, other
    both = jnp.where(core == 0, jnp.stack([mine, other], 1), jnp.stack([other, mine], 1))
    if tie is None:
        return both.reshape((n,) + tail)
    return both.reshape((n,) + tail), tie


def reduce_kv(part):
    n = lax.axis_size("kv")
    me = lax.axis_index("kv")
    bit = n // 2
    while bit >= 1:
        half = part.shape[0] // 2
        high = (me & bit) != 0
        keep = jnp.where(high, part[half:], part[:half])
        send = jnp.where(high, part[:half], part[half:])
        part = keep + lax.ppermute(send, "kv", [(i, i ^ bit) for i in range(n)])
        bit //= 2
    return part


def block_tables(block_lists, shard_first, blocks_here):
    below = jnp.sum((block_lists < shard_first).astype(jnp.int32), axis=-1)
    inside = jnp.sum(
        ((block_lists >= shard_first) & (block_lists < shard_first + blocks_here)).astype(
            jnp.int32
        ),
        axis=-1,
    )
    slot_ids = jnp.arange(MOST, dtype=jnp.int32)
    places = jnp.clip(below[..., None] + slot_ids, 0, block_lists.shape[-1] - 1)
    picked = jnp.take_along_axis(block_lists, places, axis=-1) - shard_first
    usable = slot_ids < inside[..., None]
    picked = jnp.where(usable, picked, 0)
    return picked, inside


def attn_kernel(picked_ref, count_ref, pos_ref, q_ref, k_ref, v_ref, part_ref, sc_ref,
                vsel_ref, w_ref, *, heads, rows, tq, score_scale):
    b = pl.program_id(0)
    h = pl.program_id(1)
    item = b * heads + h
    n = count_ref[item]
    q_t = q_ref[...].reshape(rows, HD).astype(jnp.float32).T.astype(jnp.bfloat16)
    key_ids = lax.broadcasted_iota(jnp.int32, (BLK, rows), 0)
    row_ids = lax.broadcasted_iota(jnp.int32, (BLK, rows), 1)
    tok = (row_ids // (rows // (BLK // tq))) * tq + row_ids % tq
    limit = b * BLK + tok - pos_ref[0]

    def scores(s):
        blk = picked_ref[item * MOST + s]
        start = pl.multiple_of(blk * BLK, BLK)
        kb = k_ref[pl.ds(start, BLK), :]
        return blk, jnp.dot(kb, q_t, preferred_element_type=jnp.float32)

    def first(s, m):
        blk, sc = scores(s)
        sc_ref[s] = sc
        return jnp.maximum(m, jnp.max(sc, axis=0, keepdims=True))

    last = jnp.maximum(n - 1, 0)
    m = lax.fori_loop(0, last, first, jnp.full((1, rows), -jnp.inf, jnp.float32))
    blk, sc = scores(last)
    sc = jnp.where(blk * BLK + key_ids <= limit, sc, -jnp.inf)
    sc_ref[last] = sc
    m = jnp.maximum(m, jnp.max(sc, axis=0, keepdims=True))
    peak = (m * score_scale).astype(jnp.bfloat16).astype(jnp.float32)
    offset = peak / score_scale
    factor = score_scale * math.log2(math.e)

    def second(s, tot):
        blk = picked_ref[item * MOST + s]
        start = pl.multiple_of(blk * BLK, BLK)
        vsel_ref[s] = v_ref[pl.ds(start, BLK), :]
        w = jnp.exp2((sc_ref[s] - offset) * factor)
        w_ref[s] = w.astype(jnp.bfloat16)
        return tot + jnp.sum(w, axis=0, keepdims=True)

    tot = lax.fori_loop(0, n, second, jnp.zeros((1, rows), jnp.float32))

    def blank(s, carry):
        vsel_ref[s] = jnp.zeros((BLK, HD), jnp.bfloat16)
        w_ref[s] = jnp.zeros((BLK, rows), jnp.bfloat16)
        return carry

    lax.fori_loop(n, MOST, blank, 0)
    acc = lax.dot_general(
        vsel_ref[...].reshape(MOST * BLK, HD), w_ref[...].reshape(MOST * BLK, rows),
        (((0,), (0,)), ((), ())), preferred_element_type=jnp.float32,
    )
    total = tot.astype(jnp.bfloat16).astype(jnp.float32)
    out = (acc / total).astype(jnp.bfloat16)
    slab = jnp.concatenate([peak, total], axis=0).astype(jnp.bfloat16)
    chunks = part_ref.shape[1]
    width = rows // chunks
    for head in range(heads):
        @pl.when(h == head)
        def _():
            for j in range(chunks):
                part_ref[0, j, head * HD:(head + 1) * HD, :] = out[:, j * width:(j + 1) * width]
                part_ref[0, j, heads * HD + 2 * head:heads * HD + 2 * head + 2, :] = (
                    slab[:, j * width:(j + 1) * width]
                )


def on_device(queries, key_cache, value_cache, blocks, out_weight):
    shard_count = lax.axis_size("ctx")
    here_index = lax.axis_index("ctx")
    local_heads = key_cache.shape[1] // HD
    tq = queries.shape[0]
    group_size = queries.shape[1] // (local_heads * HD)
    blocks_here = key_cache.shape[0] // BLK
    query_tokens = tq * shard_count
    qblocks = query_tokens // BLK
    per_block = shard_count // qblocks
    rows = group_size * BLK
    width = rows // per_block
    slab_rows = local_heads * HD + 16
    total_keys = shard_count * key_cache.shape[0]

    block_lists = lax.dynamic_slice_in_dim(
        blocks, lax.axis_index("kv") * local_heads, local_heads, 1
    )
    shard_first = here_index * blocks_here
    picked, inside = block_tables(block_lists, shard_first, blocks_here)
    pos0 = (shard_first * BLK - (total_keys - query_tokens)).astype(jnp.int32).reshape(1)

    qt = queries.reshape(tq, local_heads * group_size, HD).transpose(1, 0, 2)
    tables = (picked.reshape(-1).astype(jnp.int32), inside.reshape(-1).astype(jnp.int32), pos0)
    q_all, tables = gather_ctx(qt, tables)
    q_all = q_all.reshape(qblocks, per_block, local_heads, group_size, tq, HD)

    kernel = functools.partial(
        attn_kernel, heads=local_heads, rows=rows, tq=tq, score_scale=1.0 / math.sqrt(HD)
    )
    grid_spec = pltpu.PrefetchScalarGridSpec(
        num_scalar_prefetch=3,
        grid=(qblocks, local_heads),
        in_specs=[
            pl.BlockSpec((1, per_block, 1, group_size, tq, HD),
                         lambda b, h, *_: (b, 0, h, 0, 0, 0)),
            pl.BlockSpec((key_cache.shape[0], HD), lambda b, h, *_: (0, h)),
            pl.BlockSpec((value_cache.shape[0], HD), lambda b, h, *_: (0, h)),
        ],
        out_specs=pl.BlockSpec((1, per_block, slab_rows, width),
                               lambda b, h, *_: (b, 0, 0, 0)),
        scratch_shapes=[
            pltpu.VMEM((MOST, BLK, rows), jnp.float32),
            pltpu.VMEM((MOST, BLK, HD), jnp.bfloat16),
            pltpu.VMEM((MOST, BLK, rows), jnp.bfloat16),
        ],
    )
    part = pl.pallas_call(
        kernel,
        grid_spec=grid_spec,
        out_shape=jax.ShapeDtypeStruct((qblocks, per_block, slab_rows, width), jnp.bfloat16),
        compiler_params=pltpu.CompilerParams(
            dimension_semantics=("arbitrary", "arbitrary"),
        ),
    )(*tables, q_all, key_cache, value_cache)

    part = part.reshape(shard_count, slab_rows, width)
    part_in = lax.all_to_all(part, "ctx", 0, 0, tiled=True).astype(jnp.float32)
    stats = part_in[:, local_heads * HD:local_heads * HD + 2 * local_heads, :]
    stats = stats.reshape(shard_count, local_heads, 2, width)
    peak_all = stats[:, :, 0, :]
    peak_top = jnp.max(peak_all, axis=0)
    weight_all = stats[:, :, 1, :] * jnp.exp(peak_all - peak_top)
    values_in = part_in[:, :local_heads * HD, :].reshape(shard_count, local_heads, HD, width)
    summed = jnp.sum(weight_all[:, :, None, :] * values_in, axis=0)
    merged = summed / jnp.sum(weight_all, axis=0)[:, None, :]
    merged = merged.reshape(local_heads, HD, group_size, tq).transpose(3, 0, 2, 1)
    attended_heads = merged.astype(jnp.bfloat16).reshape(tq, -1)
    mine, other = gather_ctx(attended_heads, halves=True)
    core = here_index % 2
    mine, other = (
        jnp.dot(part.reshape(-1, attended_heads.shape[1]), out_weight,
                preferred_element_type=jnp.float32).reshape(shard_count // 2, tq, -1)
        for part in (mine, other)
    )
    projected = jnp.where(
        core == 0, jnp.stack([mine, other], 1), jnp.stack([other, mine], 1)
    ).reshape(query_tokens, -1)
    return reduce_kv(projected).astype(jnp.bfloat16)


def solution(mesh):
    placed = (P("ctx", "kv"), P("ctx", "kv"), P("ctx", "kv"), P(), P("kv", "ctx"))
    return jax.shard_map(
        on_device, mesh=mesh, in_specs=placed, out_specs=P("kv", "ctx"), check_vma=False
    )
```

```python
import functools
import math

import jax
import jax.numpy as jnp
from jax import lax
from jax.experimental import pallas as pl
from jax.experimental.pallas import tpu as pltpu
from jax.sharding import PartitionSpec as P

HD = 128
BLK = 128
MOST = 7

ORDERS = ((8, 4, 32, 16, 2), (32, 8, 4, 2, 16))


def gather_ctx(x, tie=None, halves=False):
    n = lax.axis_size("ctx")
    me = lax.axis_index("ctx")
    core = me % 2
    steps = len(ORDERS[0])
    buf = x[None]
    for step in range(steps):
        a0, a1 = ORDERS[0][step], ORDERS[1][step]
        pairs = [(c, c ^ (a0 if c % 2 == 0 else a1)) for c in range(n)]
        other = lax.ppermute(buf, "ctx", pairs)
        low = (me & jnp.where(core == 0, a0, a1)) == 0
        buf = jnp.where(low, jnp.concatenate([buf, other]), jnp.concatenate([other, buf]))
        if step == 0 and tie is not None:
            buf, tie = lax.optimization_barrier((buf, tie))
    tail = buf.shape[1:]
    outs = []
    for order in ORDERS:
        dims_bits = [order[steps - 1 - d].bit_length() - 2 for d in range(steps)]
        perm = [dims_bits.index(bb) for bb in reversed(range(steps))]
        t = buf.reshape((2,) * steps + tail)
        t = t.transpose(perm + list(range(steps, steps + len(tail))))
        outs.append(t.reshape((2 ** steps,) + tail))
    mine = jnp.where(core == 0, outs[0], outs[1])
    other = lax.ppermute(mine, "ctx", [(c, c ^ 1) for c in range(n)])
    if halves:
        return mine, other
    both = jnp.where(core == 0, jnp.stack([mine, other], 1), jnp.stack([other, mine], 1))
    if tie is None:
        return both.reshape((n,) + tail)
    return both.reshape((n,) + tail), tie


def reduce_kv(part):
    n = lax.axis_size("kv")
    me = lax.axis_index("kv")
    bit = n // 2
    while bit >= 1:
        half = part.shape[0] // 2
        high = (me & bit) != 0
        keep = jnp.where(high, part[half:], part[:half])
        send = jnp.where(high, part[:half], part[half:])
        got = lax.ppermute(send.astype(jnp.bfloat16), "kv", [(i, i ^ bit) for i in range(n)])
        part = keep + got.astype(jnp.float32)
        bit //= 2
    return part


def block_tables(block_lists, shard_first, blocks_here):
    below = jnp.sum((block_lists < shard_first).astype(jnp.int32), axis=-1)
    inside = jnp.sum(
        ((block_lists >= shard_first) & (block_lists < shard_first + blocks_here)).astype(
            jnp.int32
        ),
        axis=-1,
    )
    slot_ids = jnp.arange(MOST, dtype=jnp.int32)
    places = jnp.clip(below[..., None] + slot_ids, 0, block_lists.shape[-1] - 1)
    picked = jnp.take_along_axis(block_lists, places, axis=-1) - shard_first
    usable = slot_ids < inside[..., None]
    picked = jnp.where(usable, picked, 0)
    return picked, inside


def attn_kernel(picked_ref, count_ref, pos_ref, q_ref, k_ref, v_ref, part_ref, sc_ref,
                vsel_ref, w_ref, *, heads, rows, tq, score_scale):
    b = pl.program_id(0)
    h = pl.program_id(1)
    item = b * heads + h
    n = count_ref[item]
    q_t = q_ref[...].reshape(rows, HD).astype(jnp.float32).T.astype(jnp.bfloat16)
    key_ids = lax.broadcasted_iota(jnp.int32, (BLK, rows), 0)
    row_ids = lax.broadcasted_iota(jnp.int32, (BLK, rows), 1)
    tok = (row_ids // (rows // (BLK // tq))) * tq + row_ids % tq
    limit = b * BLK + tok - pos_ref[0]

    def scores(s):
        blk = picked_ref[item * MOST + s]
        start = pl.multiple_of(blk * BLK, BLK)
        kb = k_ref[pl.ds(start, BLK), :]
        sc = jnp.dot(kb, q_t, preferred_element_type=jnp.float32)
        return blk, sc * score_scale

    def first(s, m):
        blk, sc = scores(s)
        sc_ref[s] = sc
        return jnp.maximum(m, jnp.max(sc, axis=0, keepdims=True))

    last = jnp.maximum(n - 1, 0)
    m = lax.fori_loop(0, last, first, jnp.full((1, rows), -jnp.inf, jnp.float32))
    blk, sc = scores(last)
    sc = jnp.where(blk * BLK + key_ids <= limit, sc, -jnp.inf)
    sc_ref[last] = sc
    m = jnp.maximum(m, jnp.max(sc, axis=0, keepdims=True))
    peak = m.astype(jnp.bfloat16).astype(jnp.float32)

    def second(s, tot):
        blk = picked_ref[item * MOST + s]
        start = pl.multiple_of(blk * BLK, BLK)
        vsel_ref[s] = v_ref[pl.ds(start, BLK), :]
        w = jnp.exp(sc_ref[s] - peak)
        w_ref[s] = w.astype(jnp.bfloat16)
        return tot + jnp.sum(w, axis=0, keepdims=True)

    tot = lax.fori_loop(0, n, second, jnp.zeros((1, rows), jnp.float32))

    def blank(s, carry):
        vsel_ref[s] = jnp.zeros((BLK, HD), jnp.bfloat16)
        w_ref[s] = jnp.zeros((BLK, rows), jnp.bfloat16)
        return carry

    lax.fori_loop(n, MOST, blank, 0)
    acc = lax.dot_general(
        vsel_ref[...].reshape(MOST * BLK, HD), w_ref[...].reshape(MOST * BLK, rows),
        (((0,), (0,)), ((), ())), preferred_element_type=jnp.float32,
    )
    total = tot.astype(jnp.bfloat16).astype(jnp.float32)
    out = (acc / total).astype(jnp.bfloat16)
    slab = jnp.concatenate([peak, total], axis=0).astype(jnp.bfloat16)
    chunks = part_ref.shape[1]
    width = rows // chunks
    for head in range(heads):
        @pl.when(h == head)
        def _():
            for j in range(chunks):
                part_ref[0, j, head * HD:(head + 1) * HD, :] = out[:, j * width:(j + 1) * width]
                part_ref[0, j, heads * HD + 2 * head:heads * HD + 2 * head + 2, :] = (
                    slab[:, j * width:(j + 1) * width]
                )


def on_device(queries, key_cache, value_cache, blocks, out_weight):
    shard_count = lax.axis_size("ctx")
    here_index = lax.axis_index("ctx")
    local_heads = key_cache.shape[1] // HD
    tq = queries.shape[0]
    group_size = queries.shape[1] // (local_heads * HD)
    blocks_here = key_cache.shape[0] // BLK
    query_tokens = tq * shard_count
    qblocks = query_tokens // BLK
    per_block = shard_count // qblocks
    rows = group_size * BLK
    width = rows // per_block
    slab_rows = local_heads * HD + 16
    total_keys = shard_count * key_cache.shape[0]

    block_lists = lax.dynamic_slice_in_dim(
        blocks, lax.axis_index("kv") * local_heads, local_heads, 1
    )
    shard_first = here_index * blocks_here
    picked, inside = block_tables(block_lists, shard_first, blocks_here)
    pos0 = (shard_first * BLK - (total_keys - query_tokens)).astype(jnp.int32).reshape(1)

    qt = queries.reshape(tq, local_heads * group_size, HD).transpose(1, 0, 2)
    tables = (picked.reshape(-1).astype(jnp.int32), inside.reshape(-1).astype(jnp.int32), pos0)
    q_all, tables = gather_ctx(qt, tables)
    q_all = q_all.reshape(qblocks, per_block, local_heads, group_size, tq, HD)

    kernel = functools.partial(
        attn_kernel, heads=local_heads, rows=rows, tq=tq, score_scale=1.0 / math.sqrt(HD)
    )
    grid_spec = pltpu.PrefetchScalarGridSpec(
        num_scalar_prefetch=3,
        grid=(qblocks, local_heads),
        in_specs=[
            pl.BlockSpec((1, per_block, 1, group_size, tq, HD),
                         lambda b, h, *_: (b, 0, h, 0, 0, 0)),
            pl.BlockSpec((key_cache.shape[0], HD), lambda b, h, *_: (0, h)),
            pl.BlockSpec((value_cache.shape[0], HD), lambda b, h, *_: (0, h)),
        ],
        out_specs=pl.BlockSpec((1, per_block, slab_rows, width),
                               lambda b, h, *_: (b, 0, 0, 0)),
        scratch_shapes=[
            pltpu.VMEM((MOST, BLK, rows), jnp.float32),
            pltpu.VMEM((MOST, BLK, HD), jnp.bfloat16),
            pltpu.VMEM((MOST, BLK, rows), jnp.bfloat16),
        ],
    )
    part = pl.pallas_call(
        kernel,
        grid_spec=grid_spec,
        out_shape=jax.ShapeDtypeStruct((qblocks, per_block, slab_rows, width), jnp.bfloat16),
        compiler_params=pltpu.CompilerParams(
            dimension_semantics=("arbitrary", "arbitrary"),
        ),
    )(*tables, q_all, key_cache, value_cache)

    part = part.reshape(shard_count, slab_rows, width)
    part_in = lax.all_to_all(part, "ctx", 0, 0, tiled=True).astype(jnp.float32)
    stats = part_in[:, local_heads * HD:local_heads * HD + 2 * local_heads, :]
    stats = stats.reshape(shard_count, local_heads, 2, width)
    peak_all = stats[:, :, 0, :]
    peak_top = jnp.max(peak_all, axis=0)
    weight_all = stats[:, :, 1, :] * jnp.exp(peak_all - peak_top)
    values_in = part_in[:, :local_heads * HD, :].reshape(shard_count, local_heads, HD, width)
    summed = jnp.sum(weight_all[:, :, None, :] * values_in, axis=0)
    merged = summed / jnp.sum(weight_all, axis=0)[:, None, :]
    merged = merged.reshape(local_heads, HD, group_size, tq).transpose(3, 0, 2, 1)
    attended_heads = merged.astype(jnp.bfloat16).reshape(tq, -1)
    mine, other = gather_ctx(attended_heads, halves=True)
    core = here_index % 2
    mine, other = (
        jnp.dot(part.reshape(-1, attended_heads.shape[1]), out_weight,
                preferred_element_type=jnp.float32).reshape(shard_count // 2, tq, -1)
        for part in (mine, other)
    )
    projected = jnp.where(
        core == 0, jnp.stack([mine, other], 1), jnp.stack([other, mine], 1)
    ).reshape(query_tokens, -1)
    return reduce_kv(projected).astype(jnp.bfloat16)


def solution(mesh):
    placed = (P("ctx", "kv"), P("ctx", "kv"), P("ctx", "kv"), P(), P("kv", "ctx"))
    return jax.shard_map(
        on_device, mesh=mesh, in_specs=placed, out_specs=P("kv", "ctx"), check_vma=False
    )
```

```python
import functools
import math

import jax
import jax.numpy as jnp
from jax import lax
from jax.experimental import pallas as pl
from jax.experimental.pallas import tpu as pltpu
from jax.sharding import PartitionSpec as P

HD = 128
BLK = 128
MOST = 7

ORDERS = ((8, 4, 32, 16, 2), (32, 8, 4, 2, 16))


def gather_ctx(x, tie=None, halves=False):
    n = lax.axis_size("ctx")
    me = lax.axis_index("ctx")
    core = me % 2
    steps = len(ORDERS[0])
    buf = x[None]
    for step in range(steps):
        a0, a1 = ORDERS[0][step], ORDERS[1][step]
        pairs = [(c, c ^ (a0 if c % 2 == 0 else a1)) for c in range(n)]
        other = lax.ppermute(buf, "ctx", pairs)
        low = (me & jnp.where(core == 0, a0, a1)) == 0
        buf = jnp.where(low, jnp.concatenate([buf, other]), jnp.concatenate([other, buf]))
        if step == 0 and tie is not None:
            buf, tie = lax.optimization_barrier((buf, tie))
    tail = buf.shape[1:]
    outs = []
    for order in ORDERS:
        dims_bits = [order[steps - 1 - d].bit_length() - 2 for d in range(steps)]
        perm = [dims_bits.index(bb) for bb in reversed(range(steps))]
        t = buf.reshape((2,) * steps + tail)
        t = t.transpose(perm + list(range(steps, steps + len(tail))))
        outs.append(t.reshape((2 ** steps,) + tail))
    mine = jnp.where(core == 0, outs[0], outs[1])
    other = lax.ppermute(mine, "ctx", [(c, c ^ 1) for c in range(n)])
    if halves:
        return mine, other
    both = jnp.where(core == 0, jnp.stack([mine, other], 1), jnp.stack([other, mine], 1))
    if tie is None:
        return both.reshape((n,) + tail)
    return both.reshape((n,) + tail), tie


def reduce_kv(part):
    n = lax.axis_size("kv")
    me = lax.axis_index("kv")
    bit = n // 2
    while bit >= 1:
        half = part.shape[0] // 2
        high = (me & bit) != 0
        keep = jnp.where(high, part[half:], part[:half])
        send = jnp.where(high, part[:half], part[half:])
        got = lax.ppermute(send.astype(jnp.bfloat16), "kv", [(i, i ^ bit) for i in range(n)])
        part = keep + got.astype(jnp.float32)
        bit //= 2
    return part


def block_tables(block_lists, shard_first, blocks_here):
    below = jnp.sum((block_lists < shard_first).astype(jnp.int32), axis=-1)
    inside = jnp.sum(
        ((block_lists >= shard_first) & (block_lists < shard_first + blocks_here)).astype(
            jnp.int32
        ),
        axis=-1,
    )
    slot_ids = jnp.arange(MOST, dtype=jnp.int32)
    places = jnp.clip(below[..., None] + slot_ids, 0, block_lists.shape[-1] - 1)
    picked = jnp.take_along_axis(block_lists, places, axis=-1) - shard_first
    usable = slot_ids < inside[..., None]
    picked = jnp.where(usable, picked, 0)
    return picked, inside


def attn_kernel(picked_ref, count_ref, pos_ref, q_ref, k_ref, v_ref, part_ref, sc_ref,
                vsel_ref, w_ref, *, heads, rows, tq, score_scale):
    b = pl.program_id(0)
    h = pl.program_id(1)
    item = b * heads + h
    n = count_ref[item]
    q_t = q_ref[...].reshape(rows, HD).astype(jnp.float32).T.astype(jnp.bfloat16)
    key_ids = lax.broadcasted_iota(jnp.int32, (BLK, rows), 0)
    row_ids = lax.broadcasted_iota(jnp.int32, (BLK, rows), 1)
    tok = (row_ids // (rows // (BLK // tq))) * tq + row_ids % tq
    limit = b * BLK + tok - pos_ref[0]

    def scores(s):
        blk = picked_ref[item * MOST + s]
        start = pl.multiple_of(blk * BLK, BLK)
        kb = k_ref[pl.ds(start, BLK), :]
        sc = jnp.dot(kb, q_t, preferred_element_type=jnp.float32)
        return blk, sc * score_scale

    def first(s, m):
        blk, sc = scores(s)
        sc_ref[s] = sc
        return jnp.maximum(m, jnp.max(sc, axis=0, keepdims=True))

    last = jnp.maximum(n - 1, 0)
    m = lax.fori_loop(0, last, first, jnp.full((1, rows), -jnp.inf, jnp.float32))
    blk, sc = scores(last)
    sc = jnp.where(blk * BLK + key_ids <= limit, sc, -jnp.inf)
    sc_ref[last] = sc
    m = jnp.maximum(m, jnp.max(sc, axis=0, keepdims=True))
    peak = m.astype(jnp.bfloat16).astype(jnp.float32)

    def second(s, tot):
        blk = picked_ref[item * MOST + s]
        start = pl.multiple_of(blk * BLK, BLK)
        vsel_ref[s] = v_ref[pl.ds(start, BLK), :]
        w = jnp.exp(sc_ref[s] - peak)
        w_ref[s] = w.astype(jnp.bfloat16)
        return tot + jnp.sum(w, axis=0, keepdims=True)

    tot = lax.fori_loop(0, n, second, jnp.zeros((1, rows), jnp.float32))

    def blank(s, carry):
        vsel_ref[s] = jnp.zeros((BLK, HD), jnp.bfloat16)
        w_ref[s] = jnp.zeros((BLK, rows), jnp.bfloat16)
        return carry

    lax.fori_loop(n, MOST, blank, 0)
    acc = lax.dot_general(
        vsel_ref[...].reshape(MOST * BLK, HD), w_ref[...].reshape(MOST * BLK, rows),
        (((0,), (0,)), ((), ())), preferred_element_type=jnp.float32,
    )
    total = tot.astype(jnp.bfloat16).astype(jnp.float32)
    out = (acc / total).astype(jnp.bfloat16)
    slab = jnp.concatenate([peak, total], axis=0).astype(jnp.bfloat16)
    chunks = part_ref.shape[1]
    width = rows // chunks
    for head in range(heads):
        @pl.when(h == head)
        def _():
            for j in range(chunks):
                part_ref[0, j, head * HD:(head + 1) * HD, :] = out[:, j * width:(j + 1) * width]
                part_ref[0, j, heads * HD + 2 * head:heads * HD + 2 * head + 2, :] = (
                    slab[:, j * width:(j + 1) * width]
                )


def on_device(queries, key_cache, value_cache, blocks, out_weight):
    shard_count = lax.axis_size("ctx")
    here_index = lax.axis_index("ctx")
    local_heads = key_cache.shape[1] // HD
    tq = queries.shape[0]
    group_size = queries.shape[1] // (local_heads * HD)
    blocks_here = key_cache.shape[0] // BLK
    query_tokens = tq * shard_count
    qblocks = query_tokens // BLK
    per_block = shard_count // qblocks
    rows = group_size * BLK
    width = rows // per_block
    slab_rows = local_heads * HD + 16
    total_keys = shard_count * key_cache.shape[0]

    block_lists = lax.dynamic_slice_in_dim(
        blocks, lax.axis_index("kv") * local_heads, local_heads, 1
    )
    shard_first = here_index * blocks_here
    picked, inside = block_tables(block_lists, shard_first, blocks_here)
    pos0 = (shard_first * BLK - (total_keys - query_tokens)).astype(jnp.int32).reshape(1)

    qt = queries.reshape(tq, local_heads * group_size, HD).transpose(1, 0, 2)
    tables = (picked.reshape(-1).astype(jnp.int32), inside.reshape(-1).astype(jnp.int32), pos0)
    q_all, tables = gather_ctx(qt, tables)
    q_all = q_all.reshape(qblocks, per_block, local_heads, group_size, tq, HD)

    kernel = functools.partial(
        attn_kernel, heads=local_heads, rows=rows, tq=tq, score_scale=1.0 / math.sqrt(HD)
    )
    grid_spec = pltpu.PrefetchScalarGridSpec(
        num_scalar_prefetch=3,
        grid=(qblocks, local_heads),
        in_specs=[
            pl.BlockSpec((1, per_block, 1, group_size, tq, HD),
                         lambda b, h, *_: (b, 0, h, 0, 0, 0)),
            pl.BlockSpec((key_cache.shape[0], HD), lambda b, h, *_: (0, h)),
            pl.BlockSpec((value_cache.shape[0], HD), lambda b, h, *_: (0, h)),
        ],
        out_specs=pl.BlockSpec((1, per_block, slab_rows, width),
                               lambda b, h, *_: (b, 0, 0, 0)),
        scratch_shapes=[
            pltpu.VMEM((MOST, BLK, rows), jnp.float32),
            pltpu.VMEM((MOST, BLK, HD), jnp.bfloat16),
            pltpu.VMEM((MOST, BLK, rows), jnp.bfloat16),
        ],
    )
    part = pl.pallas_call(
        kernel,
        grid_spec=grid_spec,
        out_shape=jax.ShapeDtypeStruct((qblocks, per_block, slab_rows, width), jnp.bfloat16),
        compiler_params=pltpu.CompilerParams(
            dimension_semantics=("arbitrary", "arbitrary"),
        ),
    )(*tables, q_all, key_cache, value_cache)

    part = part.reshape(shard_count, slab_rows, width)
    part_in = lax.all_to_all(part, "ctx", 0, 0, tiled=True)
    stats = part_in[:, local_heads * HD:local_heads * HD + 2 * local_heads, :].astype(jnp.float32)
    stats = stats.reshape(shard_count, local_heads, 2, width)
    peak_all = stats[:, :, 0, :]
    peak_top = jnp.max(peak_all, axis=0)
    weight_all = stats[:, :, 1, :] * jnp.exp(peak_all - peak_top)
    values_in = part_in[:, :local_heads * HD, :].astype(jnp.float32)
    values_in = values_in.reshape(shard_count, local_heads, HD, width)
    summed = jnp.sum(weight_all[:, :, None, :] * values_in, axis=0)
    merged = summed / jnp.sum(weight_all, axis=0)[:, None, :]
    merged = merged.reshape(local_heads, HD, group_size, tq).transpose(3, 0, 2, 1)
    attended_heads = merged.astype(jnp.bfloat16).reshape(tq, -1)
    mine, other = gather_ctx(attended_heads, halves=True)
    core = here_index % 2
    mine, other = (
        jnp.dot(part.reshape(-1, attended_heads.shape[1]), out_weight,
                preferred_element_type=jnp.float32).reshape(shard_count // 2, tq, -1)
        for part in (mine, other)
    )
    projected = jnp.where(
        core == 0, jnp.stack([mine, other], 1), jnp.stack([other, mine], 1)
    ).reshape(query_tokens, -1)
    return reduce_kv(projected).astype(jnp.bfloat16)


def solution(mesh):
    placed = (P("ctx", "kv"), P("ctx", "kv"), P("ctx", "kv"), P(), P("kv", "ctx"))
    return jax.shard_map(
        on_device, mesh=mesh, in_specs=placed, out_specs=P("kv", "ctx"), check_vma=False
    )
```
